32 devices in a mesh: tm: 4 (over y, x), sta: 8 (over z, core).
Axes of the slice: x: 2, y: 2, z: 4, core: 2. Of those that a mesh axis runs over, the one named last changes fastest.
Arguments:
- records: float32 [320, 64, 4096], P('sta', 'tm'), may hold values from -480 to 480
- partners: int32 [8, 5], P('sta'), may hold values from 0 to 7, as said below
- counts: int32 [8], P('sta'), may hold values from 1 to 5, as said below
Outputs:
- cross: float32 [8, 5, 40, 10240], P('sta', None, None, 'tm')
The draws below stay inside these ranges and needn't reach their ends.
Inputs may be any that keep to these rules, and one draw needn't show every extreme that they name: `partners`: row i lists distinct blocks j with |i - j| <= 2 in its first counts[i] slots, in no particular order; the later slots hold i itself. counts[i] is at most the number of blocks j with |i - j| <= 2; some block has 5.
All inputs are finite; a program needn't handle non-finite values.
Results may differ from the reference program's by a relative error of at most 0.00077.
Values may be sent and summed in bfloat16 or wider, within the bound.
No kernel may reach another device: no remote copies, remote signals or barrier semaphores. Data moves between devices by JAX's collectives and lax.ppermute only.
A program may use at most 128 MiB of HBM per device.

```python
import math
import jax
import jax.numpy as jnp
from jax import lax

SB = 40
SAMP = 4096
BINS = 128
R = 2
MAXP = 5
BLOCKS = 8
STATIONS = 320
WINDOWS = 64


def pair_tables(key):
    folded = jax.random.fold_in(key, 11)
    block_ids = jnp.arange(BLOCKS, dtype=jnp.int32)
    offsets = jnp.arange(2 * R + 1, dtype=jnp.int32) - R
    target = block_ids[:, None] + offsets[None, :]
    inside = (target >= 0) & (target < BLOCKS)
    available = jnp.sum(inside.astype(jnp.int32), axis=1)
    counted = jax.random.randint(jax.random.fold_in(folded, 1), (BLOCKS,), 1, available + 1)
    chosen = jax.random.randint(jax.random.fold_in(folded, 2), (), R, BLOCKS - R)
    counted = jnp.where(block_ids == chosen, MAXP, counted)
    ranking = jax.vmap(lambda sub: jax.random.permutation(sub, 2 * R + 1))(jax.random.split(jax.random.fold_in(folded, 3), BLOCKS))
    scores = ranking.astype(jnp.int32) + jnp.where(inside, 0, 2 * R + 1)
    ordering = jnp.argsort(scores, axis=1, stable=True)
    paired = block_ids[:, None] + offsets[ordering]
    slot_ids = jnp.arange(MAXP, dtype=jnp.int32)
    paired = jnp.where(slot_ids[None, :] < counted[:, None], paired, block_ids[:, None])
    return (paired.astype(jnp.int32), counted.astype(jnp.int32))


def draw_partners(key, part):
    return pair_tables(key)[0]


def draw_counts(key, part):
    return pair_tables(key)[1]


def draw_records(key, part):
    subkeys = jax.random.split(jax.random.fold_in(key, 23), 6)
    noise_part = jax.random.truncated_normal(subkeys[0], -6.0, 6.0, (STATIONS, WINDOWS, SAMP), jnp.float32)
    station_gain = jnp.exp(jax.random.uniform(subkeys[1], (STATIONS, 1, 1), jnp.float32, 0.0, math.log(10.0)))
    window_gain = jnp.exp(jax.random.uniform(subkeys[2], (1, WINDOWS, 1), jnp.float32, 0.0, math.log(3.0)))
    tone_bin = jax.random.randint(subkeys[3], (STATIONS, 1, 1), 1, BINS + 1)
    tone_amp = jnp.exp(jax.random.uniform(subkeys[4], (STATIONS, 1, 1), jnp.float32, math.log(0.5), math.log(4.0)))
    phases = jax.random.uniform(subkeys[5], (STATIONS, WINDOWS, 1), jnp.float32, -math.pi, math.pi)
    positions = jnp.arange(SAMP, dtype=jnp.int32)[None, None, :]
    turns_mod = tone_bin * positions % SAMP
    tone_part = tone_amp * jnp.cos(turns_mod.astype(jnp.float32) * (2.0 * math.pi / SAMP) + phases)
    return station_gain * window_gain * (noise_part + tone_part)


def setup_inputs(seed: int = 0) -> dict:
    arg_keys = jax.random.split(jax.random.key(seed), 4)
    records = draw_records(jax.random.fold_in(arg_keys[3], 71), 0)
    partners = draw_partners(jax.random.fold_in(arg_keys[3], 71), 0)
    counts = draw_counts(jax.random.fold_in(arg_keys[3], 71), 0)
    return {"records": records, "partners": partners, "counts": counts}


def dft_columns(samples, bins):
    positions = jnp.arange(samples, dtype=jnp.int32)
    harmonic = jnp.arange(bins, dtype=jnp.int32) + 1
    phases = positions[:, None] * harmonic[None, :] % samples
    angles = phases.astype(jnp.float32) * (2.0 * math.pi / samples)
    return jnp.concatenate([jnp.cos(angles), -jnp.sin(angles)], axis=1)

def reference(records, partners, counts):
    dft_table = dft_columns(SAMP, BINS)
    blocks = records.reshape(BLOCKS, SB, WINDOWS, SAMP)

    def one_block(samples_in):
        spectra = jnp.einsum('swn,nk->wks', samples_in, dft_table, precision=lax.Precision.HIGHEST)
        mean_power = lax.optimization_barrier(jnp.mean(spectra * spectra, axis=1, keepdims=True))
        return (spectra / jnp.sqrt(mean_power + 1e-06)).astype(jnp.bfloat16)
    spectra = lax.map(one_block, blocks).reshape(BLOCKS, WINDOWS, 2, BINS, SB)
    slot_ids = jnp.arange(MAXP, dtype=jnp.int32)

    def block_cross(block_id):
        own_spec = spectra[block_id].astype(jnp.float32)
        partner_spec = spectra[partners[block_id]].astype(jnp.float32)
        real_part = jnp.einsum('wbs,pwbt->psbt', own_spec[:, 0], partner_spec[:, :, 0]) + jnp.einsum('wbs,pwbt->psbt', own_spec[:, 1], partner_spec[:, :, 1])
        imag_part = jnp.einsum('wbs,pwbt->psbt', own_spec[:, 0], partner_spec[:, :, 1]) - jnp.einsum('wbs,pwbt->psbt', own_spec[:, 1], partner_spec[:, :, 0])
        combined = jnp.stack([real_part, imag_part], axis=3).reshape(MAXP, SB, BINS * 2 * SB)
        live_slots = slot_ids < counts[block_id]
        return jnp.where(live_slots[:, None, None], combined, jnp.float32(0.0)) / WINDOWS
    return lax.map(block_cross, jnp.arange(BLOCKS, dtype=jnp.int32))
```

```python
import math

import jax
import jax.numpy as jnp
from jax import lax
from jax.experimental import pallas as pl
from jax.sharding import PartitionSpec as P

BINS = 128
R = 2
BINS_PER_STEP = 8


def passed_along(array, axis, by):
    peers = lax.axis_size(axis)
    pairs = [(i, i + by) for i in range(peers) if 0 <= i + by < peers]
    return lax.ppermute(array, axis, pairs)


def dft_columns(samples, bins, groups):
    local = bins // groups
    column = jnp.arange(2 * bins, dtype=jnp.int32)
    group_of = column // (2 * local)
    part_of = column // local % 2
    harmonic = group_of * local + column % local + 1
    positions = jnp.arange(samples, dtype=jnp.int32)
    phases = positions[:, None] * harmonic[None, :] % samples
    angles = phases.astype(jnp.float32) * (2.0 * math.pi / samples)
    return jnp.where(part_of[None, :] == 0, jnp.cos(angles), -jnp.sin(angles))


def whiten(records, groups):
    dft_table = dft_columns(records.shape[2], BINS, groups)
    spectra = jnp.einsum("swn,nk->swk", records, dft_table, precision=lax.Precision.HIGHEST)
    mean_power = jnp.mean(spectra * spectra, axis=2, keepdims=True)
    white = (spectra / jnp.sqrt(mean_power + 1e-06)).astype(jnp.bfloat16)
    return white.reshape(1, records.shape[0], records.shape[1], groups, 2 * (BINS // groups))


def cross_kernel(scale, lx_ref, y_ref, o_ref):
    bins, two_s, _ = lx_ref.shape
    s = two_s // 2
    slots = y_ref.shape[1] // s
    for b in range(bins):
        r = lax.dot_general(
            lx_ref[b], y_ref[b], (((1,), (1,)), ((), ())), preferred_element_type=jnp.float32
        )
        r = r * scale
        for p in range(slots):
            for x in range(2):
                col = (2 * b + x) * s
                o_ref[p, :, col:col + s] = r[x * s:(x + 1) * s, p * s:(p + 1) * s]


def cross_block(lx, ysel, windows):
    nb, two_s, k = lx.shape
    s = two_s // 2
    slots = ysel.shape[1] // s
    step = BINS_PER_STEP
    kernel = lambda *refs: cross_kernel(1.0 / windows, *refs)
    return pl.pallas_call(
        kernel,
        grid=(nb // step,),
        in_specs=[
            pl.BlockSpec((step, two_s, k), lambda g: (g, 0, 0)),
            pl.BlockSpec((step, slots * s, k), lambda g: (g, 0, 0)),
        ],
        out_specs=pl.BlockSpec((slots, s, step * two_s), lambda g: (0, 0, g)),
        out_shape=jax.ShapeDtypeStruct((slots, s, nb * two_s), jnp.float32),
    )(lx, ysel)


def body(records, partners, counts):
    own_spec = whiten(records, lax.axis_size("tm"))
    block_index = lax.axis_index("sta")
    partner_row = partners[0]
    slots = partner_row.shape[0]
    live_slots = jnp.arange(slots, dtype=jnp.int32) < counts[0]
    regrouped = lax.all_to_all(own_spec, "tm", split_axis=3, concat_axis=2, tiled=True)
    stations, windows, width = regrouped.shape[1], regrouped.shape[2], regrouped.shape[4]
    nb = width // 2
    spec = (
        regrouped.reshape(stations, windows, 2, nb)
        .transpose(3, 0, 2, 1)
        .reshape(nb, stations, 2 * windows)
    )
    pieces = []
    for offset in range(-R, R + 1):
        pieces.append(spec if offset == 0 else passed_along(spec, "sta", -offset))
    stacked = jnp.stack(pieces, axis=1)
    where_at = jnp.clip(partner_row - block_index + R, 0, 2 * R)
    chosen = jnp.take(stacked, where_at, axis=1)
    chosen = jnp.where(live_slots[None, :, None, None], chosen, jnp.zeros((), chosen.dtype))
    ysel = chosen.reshape(nb, slots * stations, 2 * windows)
    x_re = spec[:, :, :windows]
    x_im = spec[:, :, windows:]
    lx = jnp.concatenate([spec, jnp.concatenate([-x_im, x_re], axis=2)], axis=1)
    result = cross_block(lx, ysel, windows)
    return result[None]


def solution(mesh):
    in_specs = (P("sta", "tm", None), P("sta", None), P("sta"))
    out_specs = P("sta", None, None, "tm")
    return jax.shard_map(body, mesh=mesh, in_specs=in_specs, out_specs=out_specs, check_vma=False)
```

```python
import math

import jax
import jax.numpy as jnp
from jax import lax
from jax.experimental import pallas as pl
from jax.sharding import PartitionSpec as P

BINS = 128
R = 2
BINS_PER_STEP = 8


def passed_along(array, axis, by):
    peers = lax.axis_size(axis)
    pairs = [(i, i + by) for i in range(peers) if 0 <= i + by < peers]
    return lax.ppermute(array, axis, pairs)


def dft_columns(samples, bins, groups):
    local = bins // groups
    column = jnp.arange(2 * bins, dtype=jnp.int32)
    group_of = column // (2 * local)
    part_of = column // local % 2
    harmonic = group_of * local + column % local + 1
    fine = 1 << ((samples.bit_length() - 1) // 2)
    coarse = samples // fine
    unit = 2.0 * math.pi / samples
    outer = (jnp.arange(coarse, dtype=jnp.int32)[:, None] * fine * harmonic[None, :]) % samples
    inner = (jnp.arange(fine, dtype=jnp.int32)[:, None] * harmonic[None, :]) % samples
    c1 = jnp.cos(outer.astype(jnp.float32) * unit)[:, None, :]
    s1 = jnp.sin(outer.astype(jnp.float32) * unit)[:, None, :]
    c2 = jnp.cos(inner.astype(jnp.float32) * unit)[None, :, :]
    s2 = jnp.sin(inner.astype(jnp.float32) * unit)[None, :, :]
    cosine = c1 * c2 - s1 * s2
    minus_sine = -(s1 * c2 + c1 * s2)
    table = jnp.where(part_of[None, None, :] == 0, cosine, minus_sine)
    return table.reshape(samples, 2 * bins)


def whiten(records, groups):
    dft_table = dft_columns(records.shape[2], BINS, groups)
    spectra = jnp.einsum("swn,nk->swk", records, dft_table, precision=lax.Precision.HIGHEST)
    mean_power = jnp.mean(spectra * spectra, axis=2, keepdims=True)
    white = (spectra / jnp.sqrt(mean_power + 1e-06)).astype(jnp.bfloat16)
    return white.reshape(1, records.shape[0], records.shape[1], groups, 2 * (BINS // groups))


def cross_kernel(scale, lx_ref, y_ref, o_ref):
    bins, two_s, _ = lx_ref.shape
    s = two_s // 2
    slots = y_ref.shape[1] // s
    for b in range(bins):
        r = lax.dot_general(
            lx_ref[b], y_ref[b], (((1,), (1,)), ((), ())), preferred_element_type=jnp.float32
        )
        r = r * scale
        for p in range(slots):
            for x in range(2):
                col = (2 * b + x) * s
                o_ref[p, :, col:col + s] = r[x * s:(x + 1) * s, p * s:(p + 1) * s]


def cross_block(lx, ysel, windows):
    nb, two_s, k = lx.shape
    s = two_s // 2
    slots = ysel.shape[1] // s
    step = BINS_PER_STEP
    kernel = lambda *refs: cross_kernel(1.0 / windows, *refs)
    return pl.pallas_call(
        kernel,
        grid=(nb // step,),
        in_specs=[
            pl.BlockSpec((step, two_s, k), lambda g: (g, 0, 0)),
            pl.BlockSpec((step, slots * s, k), lambda g: (g, 0, 0)),
        ],
        out_specs=pl.BlockSpec((slots, s, step * two_s), lambda g: (0, 0, g)),
        out_shape=jax.ShapeDtypeStruct((slots, s, nb * two_s), jnp.float32),
    )(lx, ysel)


def body(records, partners, counts):
    own_spec = whiten(records, lax.axis_size("tm"))
    block_index = lax.axis_index("sta")
    partner_row = partners[0]
    slots = partner_row.shape[0]
    live_slots = jnp.arange(slots, dtype=jnp.int32) < counts[0]
    regrouped = lax.all_to_all(own_spec, "tm", split_axis=3, concat_axis=2, tiled=True)
    stations, windows, width = regrouped.shape[1], regrouped.shape[2], regrouped.shape[4]
    nb = width // 2
    spec = (
        regrouped.reshape(stations, windows, 2, nb)
        .transpose(3, 0, 2, 1)
        .reshape(nb, stations, 2 * windows)
    )
    pieces = []
    for offset in range(-R, R + 1):
        pieces.append(spec if offset == 0 else passed_along(spec, "sta", -offset))
    stacked = jnp.stack(pieces, axis=1)
    where_at = jnp.clip(partner_row - block_index + R, 0, 2 * R)
    chosen = jnp.take(stacked, where_at, axis=1)
    chosen = jnp.where(live_slots[None, :, None, None], chosen, jnp.zeros((), chosen.dtype))
    ysel = chosen.reshape(nb, slots * stations, 2 * windows)
    x_re = spec[:, :, :windows]
    x_im = spec[:, :, windows:]
    lx = jnp.concatenate([spec, jnp.concatenate([-x_im, x_re], axis=2)], axis=1)
    result = cross_block(lx, ysel, windows)
    return result[None]


def solution(mesh):
    in_specs = (P("sta", "tm", None), P("sta", None), P("sta"))
    out_specs = P("sta", None, None, "tm")
    return jax.shard_map(body, mesh=mesh, in_specs=in_specs, out_specs=out_specs, check_vma=False)
```

```python
import math

import jax
import jax.numpy as jnp
from jax import lax
from jax.experimental import pallas as pl
from jax.sharding import PartitionSpec as P

BINS = 128
R = 2
BINS_PER_STEP = 8


def passed_along(array, axis, by):
    peers = lax.axis_size(axis)
    pairs = [(i, i + by) for i in range(peers) if 0 <= i + by < peers]
    return lax.ppermute(array, axis, pairs)


def dft_columns(samples, bins, groups):
    local = bins // groups
    column = jnp.arange(2 * bins, dtype=jnp.int32)
    group_of = column // (2 * local)
    part_of = column // local % 2
    harmonic = group_of * local + column % local + 1
    fine = 1 << ((samples.bit_length() - 1) // 2)
    coarse = samples // fine
    unit = 2.0 * math.pi / samples
    outer = (jnp.arange(coarse, dtype=jnp.int32)[:, None] * fine * harmonic[None, :]) % samples
    inner = (jnp.arange(fine, dtype=jnp.int32)[:, None] * harmonic[None, :]) % samples
    c1 = jnp.cos(outer.astype(jnp.float32) * unit)[:, None, :]
    s1 = jnp.sin(outer.astype(jnp.float32) * unit)[:, None, :]
    c2 = jnp.cos(inner.astype(jnp.float32) * unit)[None, :, :]
    s2 = jnp.sin(inner.astype(jnp.float32) * unit)[None, :, :]
    cosine = c1 * c2 - s1 * s2
    minus_sine = -(s1 * c2 + c1 * s2)
    table = jnp.where(part_of[None, None, :] == 0, cosine, minus_sine)
    return table.reshape(samples, 2 * bins)


def whiten(records, groups):
    dft_table = dft_columns(records.shape[2], BINS, groups)
    spectra = jnp.einsum("swn,nk->swk", records, dft_table, precision=lax.Precision.HIGH)
    mean_power = jnp.mean(spectra * spectra, axis=2, keepdims=True)
    white = (spectra / jnp.sqrt(mean_power + 1e-06)).astype(jnp.bfloat16)
    return white.reshape(1, records.shape[0], records.shape[1], groups, 2 * (BINS // groups))


def cross_kernel(scale, lx_ref, y_ref, o_ref):
    bins, two_s, _ = lx_ref.shape
    s = two_s // 2
    slots = y_ref.shape[1] // s
    for b in range(bins):
        r = lax.dot_general(
            lx_ref[b], y_ref[b], (((1,), (1,)), ((), ())), preferred_element_type=jnp.float32
        )
        r = r * scale
        for p in range(slots):
            for x in range(2):
                col = (2 * b + x) * s
                o_ref[p, :, col:col + s] = r[x * s:(x + 1) * s, p * s:(p + 1) * s]


def cross_block(lx, ysel, windows):
    nb, two_s, k = lx.shape
    s = two_s // 2
    slots = ysel.shape[1] // s
    step = BINS_PER_STEP
    kernel = lambda *refs: cross_kernel(1.0 / windows, *refs)
    return pl.pallas_call(
        kernel,
        grid=(nb // step,),
        in_specs=[
            pl.BlockSpec((step, two_s, k), lambda g: (g, 0, 0)),
            pl.BlockSpec((step, slots * s, k), lambda g: (g, 0, 0)),
        ],
        out_specs=pl.BlockSpec((slots, s, step * two_s), lambda g: (0, 0, g)),
        out_shape=jax.ShapeDtypeStruct((slots, s, nb * two_s), jnp.float32),
    )(lx, ysel)


def body(records, partners, counts):
    own_spec = whiten(records, lax.axis_size("tm"))
    block_index = lax.axis_index("sta")
    partner_row = partners[0]
    slots = partner_row.shape[0]
    live_slots = jnp.arange(slots, dtype=jnp.int32) < counts[0]
    regrouped = lax.all_to_all(own_spec, "tm", split_axis=3, concat_axis=2, tiled=True)
    stations, windows, width = regrouped.shape[1], regrouped.shape[2], regrouped.shape[4]
    nb = width // 2
    spec = (
        regrouped.reshape(stations, windows, 2, nb)
        .transpose(3, 0, 2, 1)
        .reshape(nb, stations, 2 * windows)
    )
    pieces = []
    for offset in range(-R, R + 1):
        pieces.append(spec if offset == 0 else passed_along(spec, "sta", -offset))
    stacked = jnp.stack(pieces, axis=1)
    where_at = jnp.clip(partner_row - block_index + R, 0, 2 * R)
    chosen = jnp.take(stacked, where_at, axis=1)
    chosen = jnp.where(live_slots[None, :, None, None], chosen, jnp.zeros((), chosen.dtype))
    ysel = chosen.reshape(nb, slots * stations, 2 * windows)
    x_re = spec[:, :, :windows]
    x_im = spec[:, :, windows:]
    lx = jnp.concatenate([spec, jnp.concatenate([-x_im, x_re], axis=2)], axis=1)
    result = cross_block(lx, ysel, windows)
    return result[None]


def solution(mesh):
    in_specs = (P("sta", "tm", None), P("sta", None), P("sta"))
    out_specs = P("sta", None, None, "tm")
    return jax.shard_map(body, mesh=mesh, in_specs=in_specs, out_specs=out_specs, check_vma=False)
```

```python
import math

import jax
import jax.numpy as jnp
from jax import lax
from jax.experimental import pallas as pl
from jax.sharding import PartitionSpec as P

BINS = 128
R = 2
BINS_PER_STEP = 8


def passed_along(array, axis, by):
    peers = lax.axis_size(axis)
    pairs = [(i, i + by) for i in range(peers) if 0 <= i + by < peers]
    return lax.ppermute(array, axis, pairs)


def dft_columns(samples, bins, groups):
    local = bins // groups
    column = jnp.arange(2 * bins, dtype=jnp.int32)
    group_of = column // (2 * local)
    part_of = column // local % 2
    harmonic = group_of * local + column % local + 1
    fine = 1 << ((samples.bit_length() - 1) // 2)
    coarse = samples // fine
    unit = 2.0 * math.pi / samples
    outer = (jnp.arange(coarse, dtype=jnp.int32)[:, None] * fine * harmonic[None, :]) % samples
    inner = (jnp.arange(fine, dtype=jnp.int32)[:, None] * harmonic[None, :]) % samples
    c1 = jnp.cos(outer.astype(jnp.float32) * unit)[:, None, :]
    s1 = jnp.sin(outer.astype(jnp.float32) * unit)[:, None, :]
    c2 = jnp.cos(inner.astype(jnp.float32) * unit)[None, :, :]
    s2 = jnp.sin(inner.astype(jnp.float32) * unit)[None, :, :]
    cosine = c1 * c2 - s1 * s2
    minus_sine = -(s1 * c2 + c1 * s2)
    table = jnp.where(part_of[None, None, :] == 0, cosine, minus_sine)
    return table.reshape(samples, 2 * bins)


def whiten(records, groups):
    dft_table = dft_columns(records.shape[2], BINS, groups)
    spectra = jnp.einsum("swn,nk->swk", records, dft_table, precision=lax.Precision.HIGH)
    mean_power = jnp.mean(spectra * spectra, axis=2, keepdims=True)
    white = (spectra / jnp.sqrt(mean_power + 1e-06)).astype(jnp.bfloat16)
    return white.reshape(1, records.shape[0], records.shape[1], groups, 2 * (BINS // groups))


def cross_kernel(scale, lx_ref, y_ref, o_ref):
    bins, two_s, _ = lx_ref.shape
    s = two_s // 2
    slots = y_ref.shape[1] // s
    for b in range(bins):
        r = lax.dot_general(
            lx_ref[b], y_ref[b], (((1,), (1,)), ((), ())), preferred_element_type=jnp.float32
        )
        r = r * scale
        for p in range(slots):
            for x in range(2):
                col = (2 * b + x) * s
                o_ref[p, :, col:col + s] = r[x * s:(x + 1) * s, p * s:(p + 1) * s]


def cross_block(lx, ysel, windows):
    nb, two_s, k = lx.shape
    s = two_s // 2
    slots = ysel.shape[1] // s
    step = BINS_PER_STEP
    kernel = lambda *refs: cross_kernel(1.0 / windows, *refs)
    return pl.pallas_call(
        kernel,
        grid=(nb // step,),
        in_specs=[
            pl.BlockSpec((step, two_s, k), lambda g: (g, 0, 0)),
            pl.BlockSpec((step, slots * s, k), lambda g: (g, 0, 0)),
        ],
        out_specs=pl.BlockSpec((slots, s, step * two_s), lambda g: (0, 0, g)),
        out_shape=jax.ShapeDtypeStruct((slots, s, nb * two_s), jnp.float32),
    )(lx, ysel)


def body(records, partners, counts):
    own_spec = whiten(records, lax.axis_size("tm"))
    block_index = lax.axis_index("sta")
    partner_row = partners[0]
    slots = partner_row.shape[0]
    live_slots = jnp.arange(slots, dtype=jnp.int32) < counts[0]
    groups = lax.axis_size("tm")
    group_index = lax.axis_index("tm")
    chunks = []
    for shift in range(groups):
        target = (group_index + shift) % groups
        chunk = lax.dynamic_index_in_dim(own_spec, target, axis=3, keepdims=True)
        if shift:
            pairs = [(i, (i + shift) % groups) for i in range(groups)]
            chunk = lax.ppermute(chunk, "tm", pairs)
        chunks.append(chunk)
    regrouped = jnp.concatenate(chunks, axis=2)
    stations, windows, width = regrouped.shape[1], regrouped.shape[2], regrouped.shape[4]
    nb = width // 2
    spec = (
        regrouped.reshape(stations, windows, 2, nb)
        .transpose(3, 0, 2, 1)
        .reshape(nb, stations, 2 * windows)
    )
    pieces = []
    for offset in range(-R, R + 1):
        pieces.append(spec if offset == 0 else passed_along(spec, "sta", -offset))
    stacked = jnp.stack(pieces, axis=1)
    where_at = jnp.clip(partner_row - block_index + R, 0, 2 * R)
    chosen = jnp.take(stacked, where_at, axis=1)
    chosen = jnp.where(live_slots[None, :, None, None], chosen, jnp.zeros((), chosen.dtype))
    ysel = chosen.reshape(nb, slots * stations, 2 * windows)
    x_re = spec[:, :, :windows]
    x_im = spec[:, :, windows:]
    lx = jnp.concatenate([spec, jnp.concatenate([-x_im, x_re], axis=2)], axis=1)
    result = cross_block(lx, ysel, windows)
    return result[None]


def solution(mesh):
    in_specs = (P("sta", "tm", None), P("sta", None), P("sta"))
    out_specs = P("sta", None, None, "tm")
    return jax.shard_map(body, mesh=mesh, in_specs=in_specs, out_specs=out_specs, check_vma=False)
```

```python
import math

import jax
import jax.numpy as jnp
from jax import lax
from jax.experimental import pallas as pl
from jax.experimental.pallas import tpu as pltpu
from jax.sharding import PartitionSpec as P

BINS = 128
R = 2
BINS_PER_STEP = 8


def passed_along(array, axis, by):
    peers = lax.axis_size(axis)
    pairs = [(i, i + by) for i in range(peers) if 0 <= i + by < peers]
    return lax.ppermute(array, axis, pairs)


def dft_columns(samples, bins, groups):
    local = bins // groups
    column = jnp.arange(2 * bins, dtype=jnp.int32)
    group_of = column // (2 * local)
    part_of = column // local % 2
    harmonic = group_of * local + column % local + 1
    fine = 1 << ((samples.bit_length() - 1) // 2)
    coarse = samples // fine
    unit = 2.0 * math.pi / samples
    outer = (jnp.arange(coarse, dtype=jnp.int32)[:, None] * fine * harmonic[None, :]) % samples
    inner = (jnp.arange(fine, dtype=jnp.int32)[:, None] * harmonic[None, :]) % samples
    c1 = jnp.cos(outer.astype(jnp.float32) * unit)[:, None, :]
    s1 = jnp.sin(outer.astype(jnp.float32) * unit)[:, None, :]
    c2 = jnp.cos(inner.astype(jnp.float32) * unit)[None, :, :]
    s2 = jnp.sin(inner.astype(jnp.float32) * unit)[None, :, :]
    cosine = c1 * c2 - s1 * s2
    minus_sine = -(s1 * c2 + c1 * s2)
    table = jnp.where(part_of[None, None, :] == 0, cosine, minus_sine)
    return table.reshape(samples, 2 * bins)


def whiten(records, groups):
    dft_table = dft_columns(records.shape[2], BINS, groups)
    spectra = jnp.einsum("swn,nk->swk", records, dft_table, precision=lax.Precision.HIGH)
    mean_power = jnp.mean(spectra * spectra, axis=2, keepdims=True)
    white = (spectra / jnp.sqrt(mean_power + 1e-06)).astype(jnp.bfloat16)
    return white.reshape(1, records.shape[0], records.shape[1], groups, 2 * (BINS // groups))


def cross_kernel(scale, sel_ref, lx_ref, *refs):
    *y_refs, o_ref = refs
    bins, two_s, _ = lx_ref.shape
    s = two_s // 2
    slots = o_ref.shape[0]
    for j in range(bins // 2):
        picked = []
        for p in range(slots):
            y = jnp.zeros(y_refs[0].shape[1:], y_refs[0].dtype)
            for o, y_ref in enumerate(y_refs):
                y = jnp.where(sel_ref[p] == o, y_ref[j], y)
            picked.append(y)
        ycat = jnp.concatenate(picked, axis=0)
        for h in range(2):
            b = 2 * j + h
            r = lax.dot_general(
                lx_ref[b], ycat, (((1,), (1,)), ((), ())), preferred_element_type=jnp.float32
            )
            r = r * scale
            for p in range(slots):
                src = (2 * p + h) * s
                for x in range(2):
                    col = (2 * b + x) * s
                    o_ref[p, :, col:col + s] = r[x * s:(x + 1) * s, src:src + s]


def cross_block(sel, lx, ys, windows, slots):
    nb, two_s, k = lx.shape
    s = two_s // 2
    step = BINS_PER_STEP
    kernel = lambda *refs: cross_kernel(1.0 / windows, *refs)
    y_spec = pl.BlockSpec((step // 2, two_s, k), lambda g, sel: (g, 0, 0))
    grid_spec = pltpu.PrefetchScalarGridSpec(
        num_scalar_prefetch=1,
        grid=(nb // step,),
        in_specs=[pl.BlockSpec((step, two_s, k), lambda g, sel: (g, 0, 0))] + [y_spec] * len(ys),
        out_specs=pl.BlockSpec((slots, s, step * two_s), lambda g, sel: (0, 0, g)),
    )
    return pl.pallas_call(
        kernel,
        grid_spec=grid_spec,
        out_shape=jax.ShapeDtypeStruct((slots, s, nb * two_s), jnp.float32),
    )(sel, lx, *ys)


def body(records, partners, counts):
    own_spec = whiten(records, lax.axis_size("tm"))
    block_index = lax.axis_index("sta")
    partner_row = partners[0]
    slots = partner_row.shape[0]
    live_slots = jnp.arange(slots, dtype=jnp.int32) < counts[0]
    regrouped = lax.all_to_all(own_spec, "tm", split_axis=3, concat_axis=2, tiled=True)
    stations, windows, width = regrouped.shape[1], regrouped.shape[2], regrouped.shape[4]
    nb = width // 2
    spec = (
        regrouped.reshape(stations, windows, 2, nb)
        .transpose(3, 0, 2, 1)
        .reshape(nb, stations, 2 * windows)
    )
    paired = spec.reshape(nb // 2, 2 * stations, 2 * windows)
    ys = []
    for offset in range(-R, R + 1):
        ys.append(paired if offset == 0 else passed_along(paired, "sta", -offset))
    where_at = jnp.clip(partner_row - block_index + R, 0, 2 * R)
    sel = jnp.where(live_slots, where_at, -1).astype(jnp.int32)
    x_re = spec[:, :, :windows]
    x_im = spec[:, :, windows:]
    lx = jnp.concatenate([spec, jnp.concatenate([-x_im, x_re], axis=2)], axis=1)
    result = cross_block(sel, lx, ys, windows, slots)
    return result[None]


def solution(mesh):
    in_specs = (P("sta", "tm", None), P("sta", None), P("sta"))
    out_specs = P("sta", None, None, "tm")
    return jax.shard_map(body, mesh=mesh, in_specs=in_specs, out_specs=out_specs, check_vma=False)
```

```python
import math

import jax
import jax.numpy as jnp
from jax import lax
from jax.experimental import pallas as pl
from jax.experimental.pallas import tpu as pltpu
from jax.sharding import PartitionSpec as P

BINS = 128
R = 2
BINS_PER_STEP = 8


def passed_along(array, axis, by, sources=lambda i: True):
    peers = lax.axis_size(axis)
    pairs = [(i, i + by) for i in range(peers) if 0 <= i + by < peers and sources(i)]
    return lax.ppermute(array, axis, pairs)


def dft_columns(samples, bins, groups):
    local = bins // groups
    column = jnp.arange(2 * bins, dtype=jnp.int32)
    group_of = column // (2 * local)
    part_of = column // local % 2
    harmonic = group_of * local + column % local + 1
    fine = 1 << ((samples.bit_length() - 1) // 2)
    coarse = samples // fine
    unit = 2.0 * math.pi / samples
    outer = (jnp.arange(coarse, dtype=jnp.int32)[:, None] * fine * harmonic[None, :]) % samples
    inner = (jnp.arange(fine, dtype=jnp.int32)[:, None] * harmonic[None, :]) % samples
    c1 = jnp.cos(outer.astype(jnp.float32) * unit)[:, None, :]
    s1 = jnp.sin(outer.astype(jnp.float32) * unit)[:, None, :]
    c2 = jnp.cos(inner.astype(jnp.float32) * unit)[None, :, :]
    s2 = jnp.sin(inner.astype(jnp.float32) * unit)[None, :, :]
    cosine = c1 * c2 - s1 * s2
    minus_sine = -(s1 * c2 + c1 * s2)
    table = jnp.where(part_of[None, None, :] == 0, cosine, minus_sine)
    return table.reshape(samples, 2 * bins)


def whiten(records, groups):
    dft_table = dft_columns(records.shape[2], BINS, groups)
    spectra = jnp.einsum("swn,nk->swk", records, dft_table, precision=lax.Precision.HIGH)
    mean_power = jnp.mean(spectra * spectra, axis=2, keepdims=True)
    white = (spectra / jnp.sqrt(mean_power + 1e-06)).astype(jnp.bfloat16)
    return white.reshape(1, records.shape[0], records.shape[1], groups, 2 * (BINS // groups))


def cross_kernel(scale, sel_ref, lx_ref, *refs):
    *y_refs, o_ref = refs
    bins, two_s, _ = lx_ref.shape
    s = two_s // 2
    slots = o_ref.shape[0]
    for j in range(bins // 2):
        picked = []
        for p in range(slots):
            y = jnp.zeros(y_refs[0].shape[1:], y_refs[0].dtype)
            for o, y_ref in enumerate(y_refs):
                y = jnp.where(sel_ref[p] == o, y_ref[j], y)
            picked.append(y)
        ycat = jnp.concatenate(picked, axis=0)
        for h in range(2):
            b = 2 * j + h
            r = lax.dot_general(
                lx_ref[b], ycat, (((1,), (1,)), ((), ())), preferred_element_type=jnp.float32
            )
            r = r * scale
            for p in range(slots):
                src = (2 * p + h) * s
                for x in range(2):
                    col = (2 * b + x) * s
                    o_ref[p, :, col:col + s] = r[x * s:(x + 1) * s, src:src + s]


def cross_block(sel, lx, ys, windows, slots):
    nb, two_s, k = lx.shape
    s = two_s // 2
    step = BINS_PER_STEP
    kernel = lambda *refs: cross_kernel(1.0 / windows, *refs)
    y_spec = pl.BlockSpec((step // 2, two_s, k), lambda g, sel: (g, 0, 0))
    grid_spec = pltpu.PrefetchScalarGridSpec(
        num_scalar_prefetch=1,
        grid=(nb // step,),
        in_specs=[pl.BlockSpec((step, two_s, k), lambda g, sel: (g, 0, 0))] + [y_spec] * len(ys),
        out_specs=pl.BlockSpec((slots, s, step * two_s), lambda g, sel: (0, 0, g)),
    )
    return pl.pallas_call(
        kernel,
        grid_spec=grid_spec,
        out_shape=jax.ShapeDtypeStruct((slots, s, nb * two_s), jnp.float32),
    )(sel, lx, *ys)


def body(records, partners, counts):
    own_spec = whiten(records, lax.axis_size("tm"))
    block_index = lax.axis_index("sta")
    partner_row = partners[0]
    slots = partner_row.shape[0]
    live_slots = jnp.arange(slots, dtype=jnp.int32) < counts[0]
    regrouped = lax.all_to_all(own_spec, "tm", split_axis=3, concat_axis=2, tiled=True)
    stations, windows, width = regrouped.shape[1], regrouped.shape[2], regrouped.shape[4]
    nb = width // 2
    spec = (
        regrouped.reshape(stations, windows, 2, nb)
        .transpose(3, 0, 2, 1)
        .reshape(nb, stations, 2 * windows)
    )
    paired = spec.reshape(nb // 2, 2 * stations, 2 * windows)
    even = lambda i: i % 2 == 0
    odd = lambda i: i % 2 == 1
    left1 = passed_along(paired, "sta", 1)
    right1 = passed_along(paired, "sta", -1)
    ys = [
        passed_along(paired, "sta", 2, even),
        passed_along(left1, "sta", 1, even),
        left1,
        paired,
        right1,
        passed_along(paired, "sta", -2, odd),
        passed_along(right1, "sta", -1, odd),
    ]
    where_at = jnp.clip(partner_row - block_index + R, 0, 2 * R)
    parity = block_index % 2
    slot_ref = jnp.where(where_at == 0, parity, where_at + 1)
    slot_ref = jnp.where(where_at == 2 * R, 2 * R + 2 - parity, slot_ref)
    sel = jnp.where(live_slots, slot_ref, -1).astype(jnp.int32)
    x_re = spec[:, :, :windows]
    x_im = spec[:, :, windows:]
    lx = jnp.concatenate([spec, jnp.concatenate([-x_im, x_re], axis=2)], axis=1)
    result = cross_block(sel, lx, ys, windows, slots)
    return result[None]


def solution(mesh):
    in_specs = (P("sta", "tm", None), P("sta", None), P("sta"))
    out_specs = P("sta", None, None, "tm")
    return jax.shard_map(body, mesh=mesh, in_specs=in_specs, out_specs=out_specs, check_vma=False)
```

```python
import math

import jax
import jax.numpy as jnp
from jax import lax
from jax.experimental import pallas as pl
from jax.experimental.pallas import tpu as pltpu
from jax.sharding import PartitionSpec as P

BINS = 128
R = 2
BINS_PER_STEP = 8


def passed_along(array, axis, by, sources=lambda i: True):
    peers = lax.axis_size(axis)
    pairs = [(i, i + by) for i in range(peers) if 0 <= i + by < peers and sources(i)]
    return lax.ppermute(array, axis, pairs)


def dft_columns(samples, bins, groups):
    local = bins // groups
    column = jnp.arange(2 * bins, dtype=jnp.int32)
    group_of = column // (2 * local)
    part_of = column // local % 2
    harmonic = group_of * local + column % local + 1
    fine = 1 << ((samples.bit_length() - 1) // 2)
    coarse = samples // fine
    unit = 2.0 * math.pi / samples
    outer = (jnp.arange(coarse, dtype=jnp.int32)[:, None] * fine * harmonic[None, :]) % samples
    inner = (jnp.arange(fine, dtype=jnp.int32)[:, None] * harmonic[None, :]) % samples
    c1 = jnp.cos(outer.astype(jnp.float32) * unit)[:, None, :]
    s1 = jnp.sin(outer.astype(jnp.float32) * unit)[:, None, :]
    c2 = jnp.cos(inner.astype(jnp.float32) * unit)[None, :, :]
    s2 = jnp.sin(inner.astype(jnp.float32) * unit)[None, :, :]
    cosine = c1 * c2 - s1 * s2
    minus_sine = -(s1 * c2 + c1 * s2)
    table = jnp.where(part_of[None, None, :] == 0, cosine, minus_sine)
    return table.reshape(samples, 2 * bins)


def whiten(records, groups):
    dft_table = dft_columns(records.shape[2], BINS, groups)
    spectra = jnp.einsum("swn,nk->swk", records, dft_table, precision=lax.Precision.HIGH)
    mean_power = jnp.mean(spectra * spectra, axis=2, keepdims=True)
    white = (spectra / jnp.sqrt(mean_power + 1e-06)).astype(jnp.bfloat16)
    return white.reshape(1, records.shape[0], records.shape[1], groups, 2 * (BINS // groups))


def cross_kernel(sel_ref, lx_ref, *refs):
    *y_refs, o_ref, pick_ref = refs
    bins, two_s, _ = lx_ref.shape
    s = two_s // 2
    slots = o_ref.shape[0]
    for p in range(slots):
        rows = slice(p * two_s, (p + 1) * two_s)
        for o, y_ref in enumerate(y_refs):
            @pl.when(sel_ref[p] == o)
            def _():
                pick_ref[:, rows, :] = y_ref[...]

        @pl.when(sel_ref[p] < 0)
        def _():
            pick_ref[:, rows, :] = jnp.zeros(y_refs[0].shape, y_refs[0].dtype)

    for j in range(bins // 2):
        ycat = pick_ref[j]
        for h in range(2):
            b = 2 * j + h
            r = lax.dot_general(
                lx_ref[b], ycat, (((1,), (1,)), ((), ())), preferred_element_type=jnp.float32
            )
            for p in range(slots):
                src = (2 * p + h) * s
                for x in range(2):
                    col = (2 * b + x) * s
                    o_ref[p, :, col:col + s] = r[x * s:(x + 1) * s, src:src + s]


def cross_block(sel, lx, ys, windows, slots):
    nb, two_s, k = lx.shape
    s = two_s // 2
    step = BINS_PER_STEP
    y_spec = pl.BlockSpec((step // 2, two_s, k), lambda g, sel: (g, 0, 0))
    grid_spec = pltpu.PrefetchScalarGridSpec(
        num_scalar_prefetch=1,
        grid=(nb // step,),
        in_specs=[pl.BlockSpec((step, two_s, k), lambda g, sel: (g, 0, 0))] + [y_spec] * len(ys),
        out_specs=pl.BlockSpec((slots, s, step * two_s), lambda g, sel: (0, 0, g)),
        scratch_shapes=[pltpu.VMEM((step // 2, slots * two_s, k), lx.dtype)],
    )
    return pl.pallas_call(
        cross_kernel,
        grid_spec=grid_spec,
        out_shape=jax.ShapeDtypeStruct((slots, s, nb * two_s), jnp.float32),
    )(sel, lx, *ys)


def body(records, partners, counts):
    own_spec = whiten(records, lax.axis_size("tm"))
    block_index = lax.axis_index("sta")
    partner_row = partners[0]
    slots = partner_row.shape[0]
    live_slots = jnp.arange(slots, dtype=jnp.int32) < counts[0]
    regrouped = lax.all_to_all(own_spec, "tm", split_axis=3, concat_axis=2, tiled=True)
    stations, windows, width = regrouped.shape[1], regrouped.shape[2], regrouped.shape[4]
    nb = width // 2
    spec = (
        regrouped.reshape(stations, windows, 2, nb)
        .transpose(3, 0, 2, 1)
        .reshape(nb, stations, 2 * windows)
    )
    paired = spec.reshape(nb // 2, 2 * stations, 2 * windows)
    even = lambda i: i % 2 == 0
    odd = lambda i: i % 2 == 1
    left1 = passed_along(paired, "sta", 1)
    right1 = passed_along(paired, "sta", -1)
    ys = [
        passed_along(paired, "sta", 2, even),
        passed_along(left1, "sta", 1, even),
        left1,
        paired,
        right1,
        passed_along(paired, "sta", -2, odd),
        passed_along(right1, "sta", -1, odd),
    ]
    where_at = jnp.clip(partner_row - block_index + R, 0, 2 * R)
    parity = block_index % 2
    slot_ref = jnp.where(where_at == 0, parity, where_at + 1)
    slot_ref = jnp.where(where_at == 2 * R, 2 * R + 2 - parity, slot_ref)
    sel = jnp.where(live_slots, slot_ref, -1).astype(jnp.int32)
    x_re = spec[:, :, :windows]
    x_im = spec[:, :, windows:]
    lx = jnp.concatenate([spec, jnp.concatenate([-x_im, x_re], axis=2)], axis=1)
    lx = lx * jnp.asarray(1.0 / windows, lx.dtype)
    result = cross_block(sel, lx, ys, windows, slots)
    return result[None]


def solution(mesh):
    in_specs = (P("sta", "tm", None), P("sta", None), P("sta"))
    out_specs = P("sta", None, None, "tm")
    return jax.shard_map(body, mesh=mesh, in_specs=in_specs, out_specs=out_specs, check_vma=False)
```

```python
import math

import jax
import jax.numpy as jnp
from jax import lax
from jax.experimental import pallas as pl
from jax.experimental.pallas import tpu as pltpu
from jax.sharding import PartitionSpec as P

BINS = 128
R = 2
BINS_PER_STEP = 8


def passed_along(array, axis, by, sources=lambda i: True):
    peers = lax.axis_size(axis)
    pairs = [(i, i + by) for i in range(peers) if 0 <= i + by < peers and sources(i)]
    return lax.ppermute(array, axis, pairs)


def dft_factors(samples, bins, groups):
    local = bins // groups
    column = jnp.arange(2 * bins, dtype=jnp.int32)
    group_of = column // (2 * local)
    part_of = column // local % 2
    harmonic = group_of * local + column % local + 1
    fine = 1 << ((samples.bit_length() - 1) // 2)
    coarse = samples // fine
    unit = 2.0 * math.pi / samples
    outer = (jnp.arange(coarse, dtype=jnp.int32)[:, None] * fine * harmonic[None, :]) % samples
    inner = (jnp.arange(fine, dtype=jnp.int32)[:, None] * harmonic[None, :]) % samples
    c1 = jnp.cos(outer.astype(jnp.float32) * unit)
    s1 = jnp.sin(outer.astype(jnp.float32) * unit)
    c2 = jnp.cos(inner.astype(jnp.float32) * unit)
    s2 = jnp.sin(inner.astype(jnp.float32) * unit)
    is_cos = part_of[None, :] == 0
    p1 = jnp.where(is_cos, c1, -s1)
    q1 = jnp.where(is_cos, -s1, -c1)
    return p1, q1, c2, s2


def split_bf16(v):
    hi = v.astype(jnp.bfloat16)
    lo = (v - hi.astype(jnp.float32)).astype(jnp.bfloat16)
    return hi, lo


def dft_kernel(p1_ref, q1_ref, c2_ref, s2_ref, x_ref, o_ref, acc_ref):
    k = pl.program_id(0)

    @pl.when(k == 0)
    def _():
        acc_ref[...] = jnp.zeros(acc_ref.shape, acc_ref.dtype)

    c2 = c2_ref[...]
    s2 = s2_ref[...]
    rows = [p1_ref[a:a + 1, :] * c2 + q1_ref[a:a + 1, :] * s2 for a in range(p1_ref.shape[0])]
    t_hi, t_lo = split_bf16(jnp.concatenate(rows, axis=0))
    x_hi, x_lo = split_bf16(x_ref[...])
    dot = lambda a, b: jnp.dot(a, b, preferred_element_type=jnp.float32)
    acc_ref[...] += dot(x_hi, t_hi) + dot(x_hi, t_lo) + dot(x_lo, t_hi)

    @pl.when(k == pl.num_programs(0) - 1)
    def _():
        spectra = acc_ref[...]
        mean_power = jnp.mean(spectra * spectra, axis=1, keepdims=True)
        o_ref[...] = (spectra / jnp.sqrt(mean_power + 1e-06)).astype(o_ref.dtype)


def whiten(records, groups):
    stations, windows, samples = records.shape
    p1, q1, c2, s2 = dft_factors(samples, BINS, groups)
    fine, width = c2.shape
    coarse_step = 8
    rows = stations * windows
    x = records.reshape(rows, samples)
    white = pl.pallas_call(
        dft_kernel,
        grid=(samples // (fine * coarse_step),),
        in_specs=[
            pl.BlockSpec((coarse_step, width), lambda k: (k, 0)),
            pl.BlockSpec((coarse_step, width), lambda k: (k, 0)),
            pl.BlockSpec((fine, width), lambda k: (0, 0)),
            pl.BlockSpec((fine, width), lambda k: (0, 0)),
            pl.BlockSpec((rows, fine * coarse_step), lambda k: (0, k)),
        ],
        out_specs=pl.BlockSpec((rows, width), lambda k: (0, 0)),
        out_shape=jax.ShapeDtypeStruct((rows, width), jnp.bfloat16),
        scratch_shapes=[pltpu.VMEM((rows, width), jnp.float32)],
    )(p1, q1, c2, s2, x)
    return white.reshape(1, stations, windows, groups, width // groups)


def cross_kernel(scale, sel_ref, lx_ref, *refs):
    *y_refs, o_ref = refs
    bins, two_s, _ = lx_ref.shape
    s = two_s // 2
    slots = o_ref.shape[0]
    for j in range(bins // 2):
        picked = []
        for p in range(slots):
            y = jnp.zeros(y_refs[0].shape[1:], y_refs[0].dtype)
            for o, y_ref in enumerate(y_refs):
                y = jnp.where(sel_ref[p] == o, y_ref[j], y)
            picked.append(y)
        ycat = jnp.concatenate(picked, axis=0)
        for h in range(2):
            b = 2 * j + h
            r = lax.dot_general(
                lx_ref[b], ycat, (((1,), (1,)), ((), ())), preferred_element_type=jnp.float32
            )
            r = r * scale
            for p in range(slots):
                src = (2 * p + h) * s
                for x in range(2):
                    col = (2 * b + x) * s
                    o_ref[p, :, col:col + s] = r[x * s:(x + 1) * s, src:src + s]


def cross_block(sel, lx, ys, windows, slots):
    nb, two_s, k = lx.shape
    s = two_s // 2
    step = BINS_PER_STEP
    kernel = lambda *refs: cross_kernel(1.0 / windows, *refs)
    y_spec = pl.BlockSpec((step // 2, two_s, k), lambda g, sel: (g, 0, 0))
    grid_spec = pltpu.PrefetchScalarGridSpec(
        num_scalar_prefetch=1,
        grid=(nb // step,),
        in_specs=[pl.BlockSpec((step, two_s, k), lambda g, sel: (g, 0, 0))] + [y_spec] * len(ys),
        out_specs=pl.BlockSpec((slots, s, step * two_s), lambda g, sel: (0, 0, g)),
    )
    return pl.pallas_call(
        kernel,
        grid_spec=grid_spec,
        out_shape=jax.ShapeDtypeStruct((slots, s, nb * two_s), jnp.float32),
    )(sel, lx, *ys)


def body(records, partners, counts):
    own_spec = whiten(records, lax.axis_size("tm"))
    block_index = lax.axis_index("sta")
    partner_row = partners[0]
    slots = partner_row.shape[0]
    live_slots = jnp.arange(slots, dtype=jnp.int32) < counts[0]
    regrouped = lax.all_to_all(own_spec, "tm", split_axis=3, concat_axis=2, tiled=True)
    stations, windows, width = regrouped.shape[1], regrouped.shape[2], regrouped.shape[4]
    nb = width // 2
    spec = (
        regrouped.reshape(stations, windows, 2, nb)
        .transpose(3, 0, 2, 1)
        .reshape(nb, stations, 2 * windows)
    )
    paired = spec.reshape(nb // 2, 2 * stations, 2 * windows)
    even = lambda i: i % 2 == 0
    odd = lambda i: i % 2 == 1
    left1 = passed_along(paired, "sta", 1)
    right1 = passed_along(paired, "sta", -1)
    ys = [
        passed_along(paired, "sta", 2, even),
        passed_along(left1, "sta", 1, even),
        left1,
        paired,
        right1,
        passed_along(paired, "sta", -2, odd),
        passed_along(right1, "sta", -1, odd),
    ]
    where_at = jnp.clip(partner_row - block_index + R, 0, 2 * R)
    parity = block_index % 2
    slot_ref = jnp.where(where_at == 0, parity, where_at + 1)
    slot_ref = jnp.where(where_at == 2 * R, 2 * R + 2 - parity, slot_ref)
    sel = jnp.where(live_slots, slot_ref, -1).astype(jnp.int32)
    x_re = spec[:, :, :windows]
    x_im = spec[:, :, windows:]
    lx = jnp.concatenate([spec, jnp.concatenate([-x_im, x_re], axis=2)], axis=1)
    result = cross_block(sel, lx, ys, windows, slots)
    return result[None]


def solution(mesh):
    in_specs = (P("sta", "tm", None), P("sta", None), P("sta"))
    out_specs = P("sta", None, None, "tm")
    return jax.shard_map(body, mesh=mesh, in_specs=in_specs, out_specs=out_specs, check_vma=False)
```

```python
import math

import jax
import jax.numpy as jnp
from jax import lax
from jax.experimental import pallas as pl
from jax.experimental.pallas import tpu as pltpu
from jax.sharding import PartitionSpec as P

BINS = 128
R = 2
BINS_PER_STEP = 8


def passed_along(array, axis, by, sources=lambda i: True):
    peers = lax.axis_size(axis)
    pairs = [(i, i + by) for i in range(peers) if 0 <= i + by < peers and sources(i)]
    return lax.ppermute(array, axis, pairs)


def dft_factors(samples, bins, groups):
    local = bins // groups
    column = jnp.arange(2 * bins, dtype=jnp.int32)
    group_of = column // (2 * local)
    part_of = column // local % 2
    harmonic = group_of * local + column % local + 1
    fine = 1 << ((samples.bit_length() - 1) // 2)
    coarse = samples // fine
    unit = 2.0 * math.pi / samples
    outer = (jnp.arange(coarse, dtype=jnp.int32)[:, None] * fine * harmonic[None, :]) % samples
    inner = (jnp.arange(fine, dtype=jnp.int32)[:, None] * harmonic[None, :]) % samples
    c1 = jnp.cos(outer.astype(jnp.float32) * unit)
    s1 = jnp.sin(outer.astype(jnp.float32) * unit)
    c2 = jnp.cos(inner.astype(jnp.float32) * unit)
    s2 = jnp.sin(inner.astype(jnp.float32) * unit)
    is_cos = part_of[None, :] == 0
    p1 = jnp.where(is_cos, c1, -s1)
    q1 = jnp.where(is_cos, -s1, -c1)
    return p1, q1, c2, s2


def split_bf16(v):
    hi = v.astype(jnp.bfloat16)
    lo = (v - hi.astype(jnp.float32)).astype(jnp.bfloat16)
    return hi, lo


def dft_kernel(p1_ref, q1_ref, c2_ref, s2_ref, x_ref, o_ref, acc_ref):
    k = pl.program_id(0)

    @pl.when(k == 0)
    def _():
        acc_ref[...] = jnp.zeros(acc_ref.shape, acc_ref.dtype)

    c2 = c2_ref[...]
    s2 = s2_ref[...]
    rows = [p1_ref[a:a + 1, :] * c2 + q1_ref[a:a + 1, :] * s2 for a in range(p1_ref.shape[0])]
    t_hi, t_lo = split_bf16(jnp.concatenate(rows, axis=0))
    x_hi, x_lo = split_bf16(x_ref[...])
    dot = lambda a, b: jnp.dot(a, b, preferred_element_type=jnp.float32)
    acc_ref[...] += dot(x_hi, t_hi) + dot(x_hi, t_lo) + dot(x_lo, t_hi)

    @pl.when(k == pl.num_programs(0) - 1)
    def _():
        spectra = acc_ref[...]
        mean_power = jnp.mean(spectra * spectra, axis=1, keepdims=True)
        o_ref[...] = (spectra / jnp.sqrt(mean_power + 1e-06)).astype(o_ref.dtype)


def whiten(records, groups):
    stations, windows, samples = records.shape
    p1, q1, c2, s2 = dft_factors(samples, BINS, groups)
    fine, width = c2.shape
    coarse_step = 8
    rows = stations * windows
    x = records.reshape(rows, samples)
    white = pl.pallas_call(
        dft_kernel,
        grid=(samples // (fine * coarse_step),),
        in_specs=[
            pl.BlockSpec((coarse_step, width), lambda k: (k, 0)),
            pl.BlockSpec((coarse_step, width), lambda k: (k, 0)),
            pl.BlockSpec((fine, width), lambda k: (0, 0)),
            pl.BlockSpec((fine, width), lambda k: (0, 0)),
            pl.BlockSpec((rows, fine * coarse_step), lambda k: (0, k)),
        ],
        out_specs=pl.BlockSpec((rows, width), lambda k: (0, 0)),
        out_shape=jax.ShapeDtypeStruct((rows, width), jnp.bfloat16),
        scratch_shapes=[pltpu.VMEM((rows, width), jnp.float32)],
    )(p1, q1, c2, s2, x)
    return white.reshape(1, stations, windows, groups, width // groups)


def cross_kernel(scale, sel_ref, lx_ref, *refs):
    *y_refs, o_ref = refs
    bins, two_s, _ = lx_ref.shape
    s = two_s // 2
    slots = o_ref.shape[0]
    for j in range(bins // 2):
        picked = []
        for p in range(slots):
            y = jnp.zeros(y_refs[0].shape[1:], y_refs[0].dtype)
            for o, y_ref in enumerate(y_refs):
                y = jnp.where(sel_ref[p] == o, y_ref[j], y)
            picked.append(y)
        ycat = jnp.concatenate(picked, axis=0)
        for h in range(2):
            b = 2 * j + h
            r = lax.dot_general(
                lx_ref[b], ycat, (((1,), (1,)), ((), ())), preferred_element_type=jnp.float32
            )
            r = r * scale
            for p in range(slots):
                src = (2 * p + h) * s
                for x in range(2):
                    col = (2 * b + x) * s
                    o_ref[p, :, col:col + s] = r[x * s:(x + 1) * s, src:src + s]


def cross_block(sel, lx, ys, windows, slots):
    nb, two_s, k = lx.shape
    s = two_s // 2
    step = BINS_PER_STEP
    kernel = lambda *refs: cross_kernel(1.0 / windows, *refs)
    y_spec = pl.BlockSpec((step // 2, two_s, k), lambda g, sel: (g, 0, 0))
    grid_spec = pltpu.PrefetchScalarGridSpec(
        num_scalar_prefetch=1,
        grid=(nb // step,),
        in_specs=[pl.BlockSpec((step, two_s, k), lambda g, sel: (g, 0, 0))] + [y_spec] * len(ys),
        out_specs=pl.BlockSpec((slots, s, step * two_s), lambda g, sel: (0, 0, g)),
    )
    return pl.pallas_call(
        kernel,
        grid_spec=grid_spec,
        out_shape=jax.ShapeDtypeStruct((slots, s, nb * two_s), jnp.float32),
    )(sel, lx, *ys)


def body(records, partners, counts):
    own_spec = whiten(records, lax.axis_size("tm"))
    block_index = lax.axis_index("sta")
    partner_row = partners[0]
    slots = partner_row.shape[0]
    live_slots = jnp.arange(slots, dtype=jnp.int32) < counts[0]
    regrouped = lax.all_to_all(own_spec, "tm", split_axis=3, concat_axis=2, tiled=True)
    stations, windows, width = regrouped.shape[1], regrouped.shape[2], regrouped.shape[4]
    nb = width // 2
    spec = (
        regrouped.reshape(stations, windows, 2, nb)
        .transpose(3, 0, 2, 1)
        .reshape(nb, stations, 2 * windows)
    )
    paired = spec.reshape(nb // 2, 2 * stations, 2 * windows)
    peers = lax.axis_size("sta")
    parity = block_index % 2
    left1 = passed_along(paired, "sta", 1)
    right1 = passed_along(paired, "sta", -1)
    far = lax.ppermute(
        paired, "sta", [(i, i + 2 - 4 * (i % 2)) for i in range(peers) if 0 <= i + 2 - 4 * (i % 2) < peers]
    )
    relay = jnp.where(parity == 0, left1, right1)
    forwarded = lax.ppermute(
        relay, "sta", [(i, i + 1 - 2 * (i % 2)) for i in range(peers) if 0 <= i + 1 - 2 * (i % 2) < peers]
    )
    ys = [far, forwarded, left1, paired, right1]
    where_at = jnp.clip(partner_row - block_index + R, 0, 2 * R)
    slot_ref = jnp.where(where_at == 0, parity, where_at + 1)
    slot_ref = jnp.where(where_at == 2 * R, 1 - parity, slot_ref)
    sel = jnp.where(live_slots, slot_ref, -1).astype(jnp.int32)
    x_re = spec[:, :, :windows]
    x_im = spec[:, :, windows:]
    lx = jnp.concatenate([spec, jnp.concatenate([-x_im, x_re], axis=2)], axis=1)
    result = cross_block(sel, lx, ys, windows, slots)
    return result[None]


def solution(mesh):
    in_specs = (P("sta", "tm", None), P("sta", None), P("sta"))
    out_specs = P("sta", None, None, "tm")
    return jax.shard_map(body, mesh=mesh, in_specs=in_specs, out_specs=out_specs, check_vma=False)
```

```python
import math

import jax
import jax.numpy as jnp
from jax import lax
from jax.experimental import pallas as pl
from jax.experimental.pallas import tpu as pltpu
from jax.sharding import PartitionSpec as P

BINS = 128
R = 2
BINS_PER_STEP = 8


def passed_along(array, axis, by, sources=lambda i: True):
    peers = lax.axis_size(axis)
    pairs = [(i, i + by) for i in range(peers) if 0 <= i + by < peers and sources(i)]
    return lax.ppermute(array, axis, pairs)


def dft_factors(samples, bins, groups):
    local = bins // groups
    column = jnp.arange(2 * bins, dtype=jnp.int32)
    group_of = column // (2 * local)
    part_of = column // local % 2
    harmonic = group_of * local + column % local + 1
    fine = 1 << ((samples.bit_length() - 1) // 2)
    coarse = samples // fine
    unit = 2.0 * math.pi / samples
    outer = (jnp.arange(coarse, dtype=jnp.int32)[:, None] * fine * harmonic[None, :]) % samples
    inner = (jnp.arange(fine, dtype=jnp.int32)[:, None] * harmonic[None, :]) % samples
    c1 = jnp.cos(outer.astype(jnp.float32) * unit)
    s1 = jnp.sin(outer.astype(jnp.float32) * unit)
    c2 = jnp.cos(inner.astype(jnp.float32) * unit)
    s2 = jnp.sin(inner.astype(jnp.float32) * unit)
    is_cos = part_of[None, :] == 0
    p1 = jnp.where(is_cos, c1, -s1)
    q1 = jnp.where(is_cos, -s1, -c1)
    return p1, q1, c2, s2


def split_bf16(v):
    hi = v.astype(jnp.bfloat16)
    lo = (v - hi.astype(jnp.float32)).astype(jnp.bfloat16)
    return hi, lo


def dft_kernel(p1_ref, q1_ref, c2_ref, s2_ref, x_ref, o_ref, acc_ref):
    k = pl.program_id(0)

    @pl.when(k == 0)
    def _():
        acc_ref[...] = jnp.zeros(acc_ref.shape, acc_ref.dtype)

    c2 = c2_ref[...]
    s2 = s2_ref[...]
    rows = [p1_ref[a:a + 1, :] * c2 + q1_ref[a:a + 1, :] * s2 for a in range(p1_ref.shape[0])]
    t_hi, t_lo = split_bf16(jnp.concatenate(rows, axis=0))
    x_hi, x_lo = split_bf16(x_ref[...])
    dot = lambda a, b: jnp.dot(a, b, preferred_element_type=jnp.float32)
    acc_ref[...] += dot(x_hi, t_hi) + dot(x_hi, t_lo) + dot(x_lo, t_hi)

    @pl.when(k == pl.num_programs(0) - 1)
    def _():
        spectra = acc_ref[...]
        mean_power = jnp.mean(spectra * spectra, axis=1, keepdims=True)
        white = spectra / jnp.sqrt(mean_power + 1e-06)
        o_ref[...] = white.T.astype(o_ref.dtype)


def whiten(records, groups):
    stations, windows, samples = records.shape
    p1, q1, c2, s2 = dft_factors(samples, BINS, groups)
    fine, width = c2.shape
    coarse_step = 8
    rows = stations * windows
    x = records.reshape(rows, samples)
    white = pl.pallas_call(
        dft_kernel,
        grid=(samples // (fine * coarse_step),),
        in_specs=[
            pl.BlockSpec((coarse_step, width), lambda k: (k, 0)),
            pl.BlockSpec((coarse_step, width), lambda k: (k, 0)),
            pl.BlockSpec((fine, width), lambda k: (0, 0)),
            pl.BlockSpec((fine, width), lambda k: (0, 0)),
            pl.BlockSpec((rows, fine * coarse_step), lambda k: (0, k)),
        ],
        out_specs=pl.BlockSpec((width, rows), lambda k: (0, 0)),
        out_shape=jax.ShapeDtypeStruct((width, rows), jnp.bfloat16),
        scratch_shapes=[pltpu.VMEM((rows, width), jnp.float32)],
    )(p1, q1, c2, s2, x)
    return white.reshape(groups, width // groups, rows)


def cross_kernel(scale, sel_ref, lx_ref, *refs):
    *y_refs, o_ref = refs
    bins, two_s, _ = lx_ref.shape
    s = two_s // 2
    slots = o_ref.shape[0]
    for j in range(bins // 2):
        picked = []
        for p in range(slots):
            y = jnp.zeros(y_refs[0].shape[1:], y_refs[0].dtype)
            for o, y_ref in enumerate(y_refs):
                y = jnp.where(sel_ref[p] == o, y_ref[j], y)
            picked.append(y)
        ycat = jnp.concatenate(picked, axis=0)
        for h in range(2):
            b = 2 * j + h
            r = lax.dot_general(
                lx_ref[b], ycat, (((1,), (1,)), ((), ())), preferred_element_type=jnp.float32
            )
            r = r * scale
            for p in range(slots):
                src = (2 * p + h) * s
                for x in range(2):
                    col = (2 * b + x) * s
                    o_ref[p, :, col:col + s] = r[x * s:(x + 1) * s, src:src + s]


def cross_block(sel, lx, ys, windows, slots):
    nb, two_s, k = lx.shape
    s = two_s // 2
    step = BINS_PER_STEP
    kernel = lambda *refs: cross_kernel(1.0 / windows, *refs)
    y_spec = pl.BlockSpec((step // 2, two_s, k), lambda g, sel: (g, 0, 0))
    grid_spec = pltpu.PrefetchScalarGridSpec(
        num_scalar_prefetch=1,
        grid=(nb // step,),
        in_specs=[pl.BlockSpec((step, two_s, k), lambda g, sel: (g, 0, 0))] + [y_spec] * len(ys),
        out_specs=pl.BlockSpec((slots, s, step * two_s), lambda g, sel: (0, 0, g)),
    )
    return pl.pallas_call(
        kernel,
        grid_spec=grid_spec,
        out_shape=jax.ShapeDtypeStruct((slots, s, nb * two_s), jnp.float32),
    )(sel, lx, *ys)


def body(records, partners, counts):
    own_spec = whiten(records, lax.axis_size("tm"))
    block_index = lax.axis_index("sta")
    partner_row = partners[0]
    slots = partner_row.shape[0]
    live_slots = jnp.arange(slots, dtype=jnp.int32) < counts[0]
    regrouped = lax.all_to_all(own_spec, "tm", split_axis=0, concat_axis=0, tiled=True)
    groups = regrouped.shape[0]
    nb = regrouped.shape[1] // 2
    stations = records.shape[0]
    local_windows = records.shape[1]
    windows = groups * local_windows
    spec = (
        regrouped.reshape(groups, 2, nb, stations, local_windows)
        .transpose(2, 3, 1, 0, 4)
        .reshape(nb, stations, 2 * windows)
    )
    paired = spec.reshape(nb // 2, 2 * stations, 2 * windows)
    peers = lax.axis_size("sta")
    parity = block_index % 2
    left1 = passed_along(paired, "sta", 1)
    right1 = passed_along(paired, "sta", -1)
    far = lax.ppermute(
        paired, "sta", [(i, i + 2 - 4 * (i % 2)) for i in range(peers) if 0 <= i + 2 - 4 * (i % 2) < peers]
    )
    relay = jnp.where(parity == 0, left1, right1)
    forwarded = lax.ppermute(
        relay, "sta", [(i, i + 1 - 2 * (i % 2)) for i in range(peers) if 0 <= i + 1 - 2 * (i % 2) < peers]
    )
    ys = [far, forwarded, left1, paired, right1]
    where_at = jnp.clip(partner_row - block_index + R, 0, 2 * R)
    slot_ref = jnp.where(where_at == 0, parity, where_at + 1)
    slot_ref = jnp.where(where_at == 2 * R, 1 - parity, slot_ref)
    sel = jnp.where(live_slots, slot_ref, -1).astype(jnp.int32)
    x_re = spec[:, :, :windows]
    x_im = spec[:, :, windows:]
    lx = jnp.concatenate([spec, jnp.concatenate([-x_im, x_re], axis=2)], axis=1)
    result = cross_block(sel, lx, ys, windows, slots)
    return result[None]


def solution(mesh):
    in_specs = (P("sta", "tm", None), P("sta", None), P("sta"))
    out_specs = P("sta", None, None, "tm")
    return jax.shard_map(body, mesh=mesh, in_specs=in_specs, out_specs=out_specs, check_vma=False)
```

```python
import math

import jax
import jax.numpy as jnp
from jax import lax
from jax.experimental import pallas as pl
from jax.experimental.pallas import tpu as pltpu
from jax.sharding import PartitionSpec as P

BINS = 128
R = 2
BINS_PER_STEP = 8


def passed_along(array, axis, by, sources=lambda i: True):
    peers = lax.axis_size(axis)
    pairs = [(i, i + by) for i in range(peers) if 0 <= i + by < peers and sources(i)]
    return lax.ppermute(array, axis, pairs)


def dft_factors(samples, bins, groups):
    local = bins // groups
    column = jnp.arange(2 * bins, dtype=jnp.int32)
    group_of = column // (2 * local)
    part_of = column // local % 2
    harmonic = group_of * local + column % local + 1
    fine = 1 << ((samples.bit_length() - 1) // 2)
    coarse = samples // fine
    unit = 2.0 * math.pi / samples
    outer = (jnp.arange(coarse, dtype=jnp.int32)[:, None] * fine * harmonic[None, :]) % samples
    inner = (jnp.arange(fine, dtype=jnp.int32)[:, None] * harmonic[None, :]) % samples
    c1 = jnp.cos(outer.astype(jnp.float32) * unit)
    s1 = jnp.sin(outer.astype(jnp.float32) * unit)
    c2 = jnp.cos(inner.astype(jnp.float32) * unit)
    s2 = jnp.sin(inner.astype(jnp.float32) * unit)
    is_cos = part_of[None, :] == 0
    p1 = jnp.where(is_cos, c1, -s1)
    q1 = jnp.where(is_cos, -s1, -c1)
    return p1, q1, c2, s2


def split_bf16(v):
    hi = v.astype(jnp.bfloat16)
    lo = (v - hi.astype(jnp.float32)).astype(jnp.bfloat16)
    return hi, lo


def dft_kernel(p1_ref, q1_ref, c2_ref, s2_ref, x_ref, o_ref, acc_ref):
    k = pl.program_id(0)

    @pl.when(k == 0)
    def _():
        acc_ref[...] = jnp.zeros(acc_ref.shape, acc_ref.dtype)

    c2 = c2_ref[...]
    s2 = s2_ref[...]
    rows = [p1_ref[a:a + 1, :] * c2 + q1_ref[a:a + 1, :] * s2 for a in range(p1_ref.shape[0])]
    t_hi, t_lo = split_bf16(jnp.concatenate(rows, axis=0))
    x_hi, x_lo = split_bf16(x_ref[...])
    dot = lambda a, b: jnp.dot(a, b, preferred_element_type=jnp.float32)
    acc_ref[...] += dot(x_hi, t_hi) + dot(x_hi, t_lo) + dot(x_lo, t_hi)

    @pl.when(k == pl.num_programs(0) - 1)
    def _():
        spectra = acc_ref[...]
        mean_power = jnp.mean(spectra * spectra, axis=1, keepdims=True)
        o_ref[...] = (spectra / jnp.sqrt(mean_power + 1e-06)).astype(o_ref.dtype)


def whiten(records, groups):
    stations, windows, samples = records.shape
    p1, q1, c2, s2 = dft_factors(samples, BINS, groups)
    fine, width = c2.shape
    coarse_step = 32
    rows = stations * windows
    x = records.reshape(rows, samples)
    white = pl.pallas_call(
        dft_kernel,
        grid=(samples // (fine * coarse_step),),
        in_specs=[
            pl.BlockSpec((coarse_step, width), lambda k: (k, 0)),
            pl.BlockSpec((coarse_step, width), lambda k: (k, 0)),
            pl.BlockSpec((fine, width), lambda k: (0, 0)),
            pl.BlockSpec((fine, width), lambda k: (0, 0)),
            pl.BlockSpec((rows, fine * coarse_step), lambda k: (0, k)),
        ],
        out_specs=pl.BlockSpec((rows, width), lambda k: (0, 0)),
        out_shape=jax.ShapeDtypeStruct((rows, width), jnp.bfloat16),
        scratch_shapes=[pltpu.VMEM((rows, width), jnp.float32)],
    )(p1, q1, c2, s2, x)
    return white.reshape(1, stations, windows, groups, width // groups)


def cross_kernel(scale, sel_ref, lx_ref, *refs):
    *y_refs, o_ref = refs
    bins, two_s, _ = lx_ref.shape
    s = two_s // 2
    slots = o_ref.shape[0]
    for j in range(bins // 2):
        picked = []
        for p in range(slots):
            y = jnp.zeros(y_refs[0].shape[1:], y_refs[0].dtype)
            for o, y_ref in enumerate(y_refs):
                y = jnp.where(sel_ref[p] == o, y_ref[j], y)
            picked.append(y)
        ycat = jnp.concatenate(picked, axis=0)
        for h in range(2):
            b = 2 * j + h
            r = lax.dot_general(
                lx_ref[b], ycat, (((1,), (1,)), ((), ())), preferred_element_type=jnp.float32
            )
            r = r * scale
            for p in range(slots):
                src = (2 * p + h) * s
                for x in range(2):
                    col = (2 * b + x) * s
                    o_ref[p, :, col:col + s] = r[x * s:(x + 1) * s, src:src + s]


def cross_block(sel, lx, ys, windows, slots):
    nb, two_s, k = lx.shape
    s = two_s // 2
    step = BINS_PER_STEP
    kernel = lambda *refs: cross_kernel(1.0 / windows, *refs)
    y_spec = pl.BlockSpec((step // 2, two_s, k), lambda g, sel: (g, 0, 0))
    grid_spec = pltpu.PrefetchScalarGridSpec(
        num_scalar_prefetch=1,
        grid=(nb // step,),
        in_specs=[pl.BlockSpec((step, two_s, k), lambda g, sel: (g, 0, 0))] + [y_spec] * len(ys),
        out_specs=pl.BlockSpec((slots, s, step * two_s), lambda g, sel: (0, 0, g)),
    )
    return pl.pallas_call(
        kernel,
        grid_spec=grid_spec,
        out_shape=jax.ShapeDtypeStruct((slots, s, nb * two_s), jnp.float32),
    )(sel, lx, *ys)


def body(records, partners, counts):
    own_spec = whiten(records, lax.axis_size("tm"))
    block_index = lax.axis_index("sta")
    partner_row = partners[0]
    slots = partner_row.shape[0]
    live_slots = jnp.arange(slots, dtype=jnp.int32) < counts[0]
    regrouped = lax.all_to_all(own_spec, "tm", split_axis=3, concat_axis=2, tiled=True)
    stations, windows, width = regrouped.shape[1], regrouped.shape[2], regrouped.shape[4]
    nb = width // 2
    spec = (
        regrouped.reshape(stations, windows, 2, nb)
        .transpose(3, 0, 2, 1)
        .reshape(nb, stations, 2 * windows)
    )
    paired = spec.reshape(nb // 2, 2 * stations, 2 * windows)
    peers = lax.axis_size("sta")
    parity = block_index % 2
    left1 = passed_along(paired, "sta", 1)
    right1 = passed_along(paired, "sta", -1)
    far = lax.ppermute(
        paired, "sta", [(i, i + 2 - 4 * (i % 2)) for i in range(peers) if 0 <= i + 2 - 4 * (i % 2) < peers]
    )
    relay = jnp.where(parity == 0, left1, right1)
    forwarded = lax.ppermute(
        relay, "sta", [(i, i + 1 - 2 * (i % 2)) for i in range(peers) if 0 <= i + 1 - 2 * (i % 2) < peers]
    )
    ys = [far, forwarded, left1, paired, right1]
    where_at = jnp.clip(partner_row - block_index + R, 0, 2 * R)
    slot_ref = jnp.where(where_at == 0, parity, where_at + 1)
    slot_ref = jnp.where(where_at == 2 * R, 1 - parity, slot_ref)
    sel = jnp.where(live_slots, slot_ref, -1).astype(jnp.int32)
    x_re = spec[:, :, :windows]
    x_im = spec[:, :, windows:]
    lx = jnp.concatenate([spec, jnp.concatenate([-x_im, x_re], axis=2)], axis=1)
    result = cross_block(sel, lx, ys, windows, slots)
    return result[None]


def solution(mesh):
    in_specs = (P("sta", "tm", None), P("sta", None), P("sta"))
    out_specs = P("sta", None, None, "tm")
    return jax.shard_map(body, mesh=mesh, in_specs=in_specs, out_specs=out_specs, check_vma=False)
```

```python
import math

import jax
import numpy as np
import jax.numpy as jnp
from jax import lax
from jax.experimental import pallas as pl
from jax.experimental.pallas import tpu as pltpu
from jax.sharding import PartitionSpec as P

BINS = 128
R = 2
BINS_PER_STEP = 8


def passed_along(array, axis, by, sources=lambda i: True):
    peers = lax.axis_size(axis)
    pairs = [(i, i + by) for i in range(peers) if 0 <= i + by < peers and sources(i)]
    return lax.ppermute(array, axis, pairs)


def dft_factors(samples, bins, groups):
    local = bins // groups
    column = np.arange(2 * bins)
    group_of = column // (2 * local)
    part_of = column // local % 2
    harmonic = group_of * local + column % local + 1
    fine = 1 << ((samples.bit_length() - 1) // 2)
    coarse = samples // fine
    unit = 2.0 * math.pi / samples
    outer = (np.arange(coarse)[:, None] * fine * harmonic[None, :]) % samples * unit
    inner = (np.arange(fine)[:, None] * harmonic[None, :]) % samples * unit
    is_cos = part_of[None, :] == 0
    p1 = np.where(is_cos, np.cos(outer), -np.sin(outer))
    q1 = np.where(is_cos, -np.sin(outer), -np.cos(outer))
    c2 = np.cos(inner)
    s2 = np.sin(inner)
    return tuple(jnp.asarray(t.astype(np.float32)) for t in (p1, q1, c2, s2))


def split_bf16(v):
    hi = v.astype(jnp.bfloat16)
    lo = (v - hi.astype(jnp.float32)).astype(jnp.bfloat16)
    return hi, lo


def dft_kernel(p1_ref, q1_ref, c2_ref, s2_ref, x_ref, o_ref, acc_ref):
    k = pl.program_id(0)

    @pl.when(k == 0)
    def _():
        acc_ref[...] = jnp.zeros(acc_ref.shape, acc_ref.dtype)

    c2 = c2_ref[...]
    s2 = s2_ref[...]
    rows = [p1_ref[a:a + 1, :] * c2 + q1_ref[a:a + 1, :] * s2 for a in range(p1_ref.shape[0])]
    t_hi, t_lo = split_bf16(jnp.concatenate(rows, axis=0))
    x_hi, x_lo = split_bf16(x_ref[...])
    dot = lambda a, b: jnp.dot(a, b, preferred_element_type=jnp.float32)
    acc_ref[...] += dot(x_hi, t_hi) + dot(x_hi, t_lo) + dot(x_lo, t_hi)

    @pl.when(k == pl.num_programs(0) - 1)
    def _():
        spectra = acc_ref[...]
        mean_power = jnp.mean(spectra * spectra, axis=1, keepdims=True)
        o_ref[...] = (spectra / jnp.sqrt(mean_power + 1e-06)).astype(o_ref.dtype)


def whiten(records, groups):
    stations, windows, samples = records.shape
    p1, q1, c2, s2 = dft_factors(samples, BINS, groups)
    fine, width = c2.shape
    coarse_step = 32
    rows = stations * windows
    x = records.reshape(rows, samples)
    white = pl.pallas_call(
        dft_kernel,
        grid=(samples // (fine * coarse_step),),
        in_specs=[
            pl.BlockSpec((coarse_step, width), lambda k: (k, 0)),
            pl.BlockSpec((coarse_step, width), lambda k: (k, 0)),
            pl.BlockSpec((fine, width), lambda k: (0, 0)),
            pl.BlockSpec((fine, width), lambda k: (0, 0)),
            pl.BlockSpec((rows, fine * coarse_step), lambda k: (0, k)),
        ],
        out_specs=pl.BlockSpec((rows, width), lambda k: (0, 0)),
        out_shape=jax.ShapeDtypeStruct((rows, width), jnp.bfloat16),
        scratch_shapes=[pltpu.VMEM((rows, width), jnp.float32)],
    )(p1, q1, c2, s2, x)
    return white.reshape(1, stations, windows, groups, width // groups)


def cross_kernel(scale, sel_ref, lx_ref, *refs):
    *y_refs, o_ref = refs
    bins, two_s, _ = lx_ref.shape
    s = two_s // 2
    slots = o_ref.shape[0]
    for j in range(bins // 2):
        picked = []
        for p in range(slots):
            y = jnp.zeros(y_refs[0].shape[1:], y_refs[0].dtype)
            for o, y_ref in enumerate(y_refs):
                y = jnp.where(sel_ref[p] == o, y_ref[j], y)
            picked.append(y)
        ycat = jnp.concatenate(picked, axis=0)
        for h in range(2):
            b = 2 * j + h
            r = lax.dot_general(
                lx_ref[b], ycat, (((1,), (1,)), ((), ())), preferred_element_type=jnp.float32
            )
            r = r * scale
            for p in range(slots):
                src = (2 * p + h) * s
                for x in range(2):
                    col = (2 * b + x) * s
                    o_ref[p, :, col:col + s] = r[x * s:(x + 1) * s, src:src + s]


def cross_block(sel, lx, ys, windows, slots):
    nb, two_s, k = lx.shape
    s = two_s // 2
    step = BINS_PER_STEP
    kernel = lambda *refs: cross_kernel(1.0 / windows, *refs)
    y_spec = pl.BlockSpec((step // 2, two_s, k), lambda g, sel: (g, 0, 0))
    grid_spec = pltpu.PrefetchScalarGridSpec(
        num_scalar_prefetch=1,
        grid=(nb // step,),
        in_specs=[pl.BlockSpec((step, two_s, k), lambda g, sel: (g, 0, 0))] + [y_spec] * len(ys),
        out_specs=pl.BlockSpec((slots, s, step * two_s), lambda g, sel: (0, 0, g)),
    )
    return pl.pallas_call(
        kernel,
        grid_spec=grid_spec,
        out_shape=jax.ShapeDtypeStruct((slots, s, nb * two_s), jnp.float32),
    )(sel, lx, *ys)


def body(records, partners, counts):
    own_spec = whiten(records, lax.axis_size("tm"))
    block_index = lax.axis_index("sta")
    partner_row = partners[0]
    slots = partner_row.shape[0]
    live_slots = jnp.arange(slots, dtype=jnp.int32) < counts[0]
    regrouped = lax.all_to_all(own_spec, "tm", split_axis=3, concat_axis=2, tiled=True)
    stations, windows, width = regrouped.shape[1], regrouped.shape[2], regrouped.shape[4]
    nb = width // 2
    spec = (
        regrouped.reshape(stations, windows, 2, nb)
        .transpose(3, 0, 2, 1)
        .reshape(nb, stations, 2 * windows)
    )
    paired = spec.reshape(nb // 2, 2 * stations, 2 * windows)
    peers = lax.axis_size("sta")
    parity = block_index % 2
    left1 = passed_along(paired, "sta", 1)
    right1 = passed_along(paired, "sta", -1)
    far = lax.ppermute(
        paired, "sta", [(i, i + 2 - 4 * (i % 2)) for i in range(peers) if 0 <= i + 2 - 4 * (i % 2) < peers]
    )
    relay = jnp.where(parity == 0, left1, right1)
    forwarded = lax.ppermute(
        relay, "sta", [(i, i + 1 - 2 * (i % 2)) for i in range(peers) if 0 <= i + 1 - 2 * (i % 2) < peers]
    )
    ys = [far, forwarded, left1, paired, right1]
    where_at = jnp.clip(partner_row - block_index + R, 0, 2 * R)
    slot_ref = jnp.where(where_at == 0, parity, where_at + 1)
    slot_ref = jnp.where(where_at == 2 * R, 1 - parity, slot_ref)
    sel = jnp.where(live_slots, slot_ref, -1).astype(jnp.int32)
    x_re = spec[:, :, :windows]
    x_im = spec[:, :, windows:]
    lx = jnp.concatenate([spec, jnp.concatenate([-x_im, x_re], axis=2)], axis=1)
    result = cross_block(sel, lx, ys, windows, slots)
    return result[None]


def solution(mesh):
    in_specs = (P("sta", "tm", None), P("sta", None), P("sta"))
    out_specs = P("sta", None, None, "tm")
    return jax.shard_map(body, mesh=mesh, in_specs=in_specs, out_specs=out_specs, check_vma=False)
```

```python
import math

import jax
import numpy as np
import jax.numpy as jnp
from jax import lax
from jax.experimental import pallas as pl
from jax.experimental.pallas import tpu as pltpu
from jax.sharding import PartitionSpec as P

BINS = 128
R = 2
BINS_PER_STEP = 8


def passed_along(array, axis, by, sources=lambda i: True):
    peers = lax.axis_size(axis)
    pairs = [(i, i + by) for i in range(peers) if 0 <= i + by < peers and sources(i)]
    return lax.ppermute(array, axis, pairs)


def dft_factors(samples, bins, groups):
    local = bins // groups
    column = np.arange(2 * bins)
    group_of = column // (2 * local)
    part_of = column // local % 2
    harmonic = group_of * local + column % local + 1
    fine = 1 << ((samples.bit_length() - 1) // 2)
    coarse = samples // fine
    unit = 2.0 * math.pi / samples
    outer = (np.arange(coarse)[:, None] * fine * harmonic[None, :]) % samples * unit
    inner = (np.arange(fine)[:, None] * harmonic[None, :]) % samples * unit
    is_cos = part_of[None, :] == 0
    p1 = np.where(is_cos, np.cos(outer), -np.sin(outer))
    q1 = np.where(is_cos, -np.sin(outer), -np.cos(outer))
    c2 = np.cos(inner)
    s2 = np.sin(inner)
    return tuple(jnp.asarray(t.astype(np.float32)) for t in (p1, q1, c2, s2))


def split_bf16(v):
    hi = v.astype(jnp.bfloat16)
    lo = (v - hi.astype(jnp.float32)).astype(jnp.bfloat16)
    return hi, lo


def dft_kernel(p1_ref, q1_ref, c2_ref, s2_ref, x_ref, o_ref, acc_ref):
    k = pl.program_id(0)

    @pl.when(k == 0)
    def _():
        acc_ref[...] = jnp.zeros(acc_ref.shape, acc_ref.dtype)

    c2 = c2_ref[...]
    s2 = s2_ref[...]
    rows = [p1_ref[a:a + 1, :] * c2 + q1_ref[a:a + 1, :] * s2 for a in range(p1_ref.shape[0])]
    t_hi, t_lo = split_bf16(jnp.concatenate(rows, axis=0))
    x_hi, x_lo = split_bf16(x_ref[...])
    dot = lambda a, b: jnp.dot(a, b, preferred_element_type=jnp.float32)
    acc_ref[...] += dot(x_hi, t_hi) + dot(x_hi, t_lo) + dot(x_lo, t_hi)

    @pl.when(k == pl.num_programs(0) - 1)
    def _():
        spectra = acc_ref[...]
        mean_power = jnp.mean(spectra * spectra, axis=1, keepdims=True)
        o_ref[...] = (spectra / jnp.sqrt(mean_power + 1e-06)).astype(o_ref.dtype)


def whiten(records, groups):
    stations, windows, samples = records.shape
    p1, q1, c2, s2 = dft_factors(samples, BINS, groups)
    fine, width = c2.shape
    coarse_step = 32
    rows = stations * windows
    x = records.reshape(rows, samples)
    white = pl.pallas_call(
        dft_kernel,
        grid=(samples // (fine * coarse_step),),
        in_specs=[
            pl.BlockSpec((coarse_step, width), lambda k: (k, 0)),
            pl.BlockSpec((coarse_step, width), lambda k: (k, 0)),
            pl.BlockSpec((fine, width), lambda k: (0, 0)),
            pl.BlockSpec((fine, width), lambda k: (0, 0)),
            pl.BlockSpec((rows, fine * coarse_step), lambda k: (0, k)),
        ],
        out_specs=pl.BlockSpec((rows, width), lambda k: (0, 0)),
        out_shape=jax.ShapeDtypeStruct((rows, width), jnp.bfloat16),
        scratch_shapes=[pltpu.VMEM((rows, width), jnp.float32)],
    )(p1, q1, c2, s2, x)
    return white.reshape(1, stations, windows, groups, width // groups)


def cross_kernel(scale, sel_ref, lx_ref, *refs):
    *y_refs, o_ref = refs
    bins, two_s, _ = lx_ref.shape
    s = two_s // 2
    slots = o_ref.shape[0]
    for j in range(bins // 2):
        picked = []
        for p in range(slots):
            y = jnp.zeros(y_refs[0].shape[1:], y_refs[0].dtype)
            for o, y_ref in enumerate(y_refs):
                y = jnp.where(sel_ref[p] == o, y_ref[j], y)
            picked.append(y)
        ycat = jnp.concatenate(picked, axis=0)
        for h in range(2):
            b = 2 * j + h
            r = lax.dot_general(
                lx_ref[b], ycat, (((1,), (1,)), ((), ())), preferred_element_type=jnp.float32
            )
            r = r * scale
            for p in range(slots):
                src = (2 * p + h) * s
                for x in range(2):
                    col = (2 * b + x) * s
                    o_ref[p, :, col:col + s] = r[x * s:(x + 1) * s, src:src + s]


def cross_block(sel, lx, ys, windows, slots):
    nb, two_s, k = lx.shape
    s = two_s // 2
    step = BINS_PER_STEP
    kernel = lambda *refs: cross_kernel(1.0 / windows, *refs)
    y_spec = pl.BlockSpec((step // 2, two_s, k), lambda g, sel: (g, 0, 0))
    grid_spec = pltpu.PrefetchScalarGridSpec(
        num_scalar_prefetch=1,
        grid=(nb // step,),
        in_specs=[pl.BlockSpec((step, two_s, k), lambda g, sel: (g, 0, 0))] + [y_spec] * len(ys),
        out_specs=pl.BlockSpec((slots, s, step * two_s), lambda g, sel: (0, 0, g)),
    )
    return pl.pallas_call(
        kernel,
        grid_spec=grid_spec,
        out_shape=jax.ShapeDtypeStruct((slots, s, nb * two_s), jnp.float32),
    )(sel, lx, *ys)


def body(records, partners, counts):
    own_spec = whiten(records, lax.axis_size("tmy") * lax.axis_size("tmx"))
    block_index = lax.axis_index("sta")
    partner_row = partners[0]
    slots = partner_row.shape[0]
    live_slots = jnp.arange(slots, dtype=jnp.int32) < counts[0]
    _, stations0, windows0, groups0, width0 = own_spec.shape
    ny = lax.axis_size("tmy")
    split = own_spec.reshape(stations0, windows0, ny, groups0 // ny, width0)
    split = lax.all_to_all(split, "tmx", split_axis=3, concat_axis=1, tiled=True)
    split = lax.all_to_all(split, "tmy", split_axis=2, concat_axis=1, tiled=True)
    regrouped = split.reshape(1, stations0, windows0 * groups0, 1, width0)
    stations, windows, width = regrouped.shape[1], regrouped.shape[2], regrouped.shape[4]
    nb = width // 2
    spec = (
        regrouped.reshape(stations, windows, 2, nb)
        .transpose(3, 0, 2, 1)
        .reshape(nb, stations, 2 * windows)
    )
    paired = spec.reshape(nb // 2, 2 * stations, 2 * windows)
    peers = lax.axis_size("sta")
    parity = block_index % 2
    left1 = passed_along(paired, "sta", 1)
    right1 = passed_along(paired, "sta", -1)
    far = lax.ppermute(
        paired, "sta", [(i, i + 2 - 4 * (i % 2)) for i in range(peers) if 0 <= i + 2 - 4 * (i % 2) < peers]
    )
    relay = jnp.where(parity == 0, left1, right1)
    forwarded = lax.ppermute(
        relay, "sta", [(i, i + 1 - 2 * (i % 2)) for i in range(peers) if 0 <= i + 1 - 2 * (i % 2) < peers]
    )
    ys = [far, forwarded, left1, paired, right1]
    where_at = jnp.clip(partner_row - block_index + R, 0, 2 * R)
    slot_ref = jnp.where(where_at == 0, parity, where_at + 1)
    slot_ref = jnp.where(where_at == 2 * R, 1 - parity, slot_ref)
    sel = jnp.where(live_slots, slot_ref, -1).astype(jnp.int32)
    x_re = spec[:, :, :windows]
    x_im = spec[:, :, windows:]
    lx = jnp.concatenate([spec, jnp.concatenate([-x_im, x_re], axis=2)], axis=1)
    result = cross_block(sel, lx, ys, windows, slots)
    return result[None]


def solution(mesh):
    tm, sta = mesh.devices.shape
    chips_x = 2 if tm % 2 == 0 else 1
    split_mesh = jax.sharding.Mesh(
        mesh.devices.reshape(tm // chips_x, chips_x, sta), ("tmy", "tmx", "sta")
    )
    tm_axes = ("tmy", "tmx")
    in_specs = (P("sta", tm_axes, None), P("sta", None), P("sta"))
    out_specs = P("sta", None, None, tm_axes)
    return jax.shard_map(body, mesh=split_mesh, in_specs=in_specs, out_specs=out_specs, check_vma=False)
```

```python
import math

import jax
import numpy as np
import jax.numpy as jnp
from jax import lax
from jax.experimental import pallas as pl
from jax.experimental.pallas import tpu as pltpu
from jax.sharding import PartitionSpec as P

BINS = 128
R = 2
BINS_PER_STEP = 8


def passed_along(array, axis, by, sources=lambda i: True):
    peers = lax.axis_size(axis)
    pairs = [(i, i + by) for i in range(peers) if 0 <= i + by < peers and sources(i)]
    return lax.ppermute(array, axis, pairs)


def dft_factors(samples, bins, groups):
    local = bins // groups
    column = np.arange(2 * bins)
    group_of = column // (2 * local)
    part_of = column // local % 2
    harmonic = group_of * local + column % local + 1
    fine = 1 << ((samples.bit_length() - 1) // 2)
    coarse = samples // fine
    unit = 2.0 * math.pi / samples
    outer = (np.arange(coarse)[:, None] * fine * harmonic[None, :]) % samples * unit
    inner = (np.arange(fine)[:, None] * harmonic[None, :]) % samples * unit
    is_cos = part_of[None, :] == 0
    p1 = np.where(is_cos, np.cos(outer), -np.sin(outer))
    q1 = np.where(is_cos, -np.sin(outer), -np.cos(outer))
    c2 = np.cos(inner)
    s2 = np.sin(inner)
    return tuple(jnp.asarray(t.astype(np.float32)) for t in (p1, q1, c2, s2))


def split_bf16(v):
    hi = v.astype(jnp.bfloat16)
    lo = (v - hi.astype(jnp.float32)).astype(jnp.bfloat16)
    return hi, lo


def dft_kernel(p1_ref, q1_ref, c2_ref, s2_ref, x_ref, o_ref, acc_ref):
    k = pl.program_id(0)

    @pl.when(k == 0)
    def _():
        acc_ref[...] = jnp.zeros(acc_ref.shape, acc_ref.dtype)

    c2 = c2_ref[...]
    s2 = s2_ref[...]
    rows = [p1_ref[a:a + 1, :] * c2 + q1_ref[a:a + 1, :] * s2 for a in range(p1_ref.shape[0])]
    t_hi, t_lo = split_bf16(jnp.concatenate(rows, axis=0))
    x_hi, x_lo = split_bf16(x_ref[...])
    dot = lambda a, b: jnp.dot(a, b, preferred_element_type=jnp.float32)
    acc_ref[...] += dot(x_hi, t_hi) + dot(x_hi, t_lo) + dot(x_lo, t_hi)

    @pl.when(k == pl.num_programs(0) - 1)
    def _():
        spectra = acc_ref[...]
        mean_power = jnp.mean(spectra * spectra, axis=1, keepdims=True)
        o_ref[...] = (spectra / jnp.sqrt(mean_power + 1e-06)).astype(o_ref.dtype)


def whiten(records, groups):
    stations, windows, samples = records.shape
    p1, q1, c2, s2 = dft_factors(samples, BINS, groups)
    fine, width = c2.shape
    coarse_step = 32
    rows = stations * windows
    x = records.reshape(rows, samples)
    white = pl.pallas_call(
        dft_kernel,
        grid=(samples // (fine * coarse_step),),
        in_specs=[
            pl.BlockSpec((coarse_step, width), lambda k: (k, 0)),
            pl.BlockSpec((coarse_step, width), lambda k: (k, 0)),
            pl.BlockSpec((fine, width), lambda k: (0, 0)),
            pl.BlockSpec((fine, width), lambda k: (0, 0)),
            pl.BlockSpec((rows, fine * coarse_step), lambda k: (0, k)),
        ],
        out_specs=pl.BlockSpec((rows, width), lambda k: (0, 0)),
        out_shape=jax.ShapeDtypeStruct((rows, width), jnp.bfloat16),
        scratch_shapes=[pltpu.VMEM((rows, width), jnp.float32)],
    )(p1, q1, c2, s2, x)
    return white.reshape(1, stations, windows, groups, width // groups)


def cross_kernel(scale, partner_ref, count_ref, lx_ref, *refs):
    *y_refs, o_ref = refs
    bins, two_s, _ = lx_ref.shape
    s = two_s // 2
    slots = o_ref.shape[0]
    block_index = lax.axis_index("sta")
    parity = block_index % 2
    sel = []
    for p in range(slots):
        where_at = jnp.clip(partner_ref[p] - block_index + R, 0, 2 * R)
        slot = jnp.where(where_at == 0, parity, where_at + 1)
        slot = jnp.where(where_at == 2 * R, 1 - parity, slot)
        sel.append(jnp.where(p < count_ref[0], slot, -1))
    for j in range(bins // 2):
        picked = []
        for p in range(slots):
            y = jnp.zeros(y_refs[0].shape[1:], y_refs[0].dtype)
            for o, y_ref in enumerate(y_refs):
                y = jnp.where(sel[p] == o, y_ref[j], y)
            picked.append(y)
        ycat = jnp.concatenate(picked, axis=0)
        for h in range(2):
            b = 2 * j + h
            r = lax.dot_general(
                lx_ref[b], ycat, (((1,), (1,)), ((), ())), preferred_element_type=jnp.float32
            )
            r = r * scale
            for p in range(slots):
                src = (2 * p + h) * s
                for x in range(2):
                    col = (2 * b + x) * s
                    o_ref[p, :, col:col + s] = r[x * s:(x + 1) * s, src:src + s]


def cross_block(partner_row, count, lx, ys, windows, slots):
    nb, two_s, k = lx.shape
    s = two_s // 2
    step = BINS_PER_STEP
    kernel = lambda *refs: cross_kernel(1.0 / windows, *refs)
    y_spec = pl.BlockSpec((step // 2, two_s, k), lambda g, *_: (g, 0, 0))
    grid_spec = pltpu.PrefetchScalarGridSpec(
        num_scalar_prefetch=2,
        grid=(nb // step,),
        in_specs=[pl.BlockSpec((step, two_s, k), lambda g, *_: (g, 0, 0))] + [y_spec] * len(ys),
        out_specs=pl.BlockSpec((slots, s, step * two_s), lambda g, *_: (0, 0, g)),
    )
    return pl.pallas_call(
        kernel,
        grid_spec=grid_spec,
        out_shape=jax.ShapeDtypeStruct((slots, s, nb * two_s), jnp.float32),
    )(partner_row, count, lx, *ys)


def body(records, partners, counts):
    own_spec = whiten(records, lax.axis_size("tm"))
    block_index = lax.axis_index("sta")
    partner_row = partners[0]
    slots = partner_row.shape[0]
    live_slots = jnp.arange(slots, dtype=jnp.int32) < counts[0]
    regrouped = lax.all_to_all(own_spec, "tm", split_axis=3, concat_axis=2, tiled=True)
    stations, windows, width = regrouped.shape[1], regrouped.shape[2], regrouped.shape[4]
    nb = width // 2
    spec = (
        regrouped.reshape(stations, windows, 2, nb)
        .transpose(3, 0, 2, 1)
        .reshape(nb, stations, 2 * windows)
    )
    paired = spec.reshape(nb // 2, 2 * stations, 2 * windows)
    peers = lax.axis_size("sta")
    parity = block_index % 2
    left1 = passed_along(paired, "sta", 1)
    right1 = passed_along(paired, "sta", -1)
    far = lax.ppermute(
        paired, "sta", [(i, i + 2 - 4 * (i % 2)) for i in range(peers) if 0 <= i + 2 - 4 * (i % 2) < peers]
    )
    relay = jnp.where(parity == 0, left1, right1)
    forwarded = lax.ppermute(
        relay, "sta", [(i, i + 1 - 2 * (i % 2)) for i in range(peers) if 0 <= i + 1 - 2 * (i % 2) < peers]
    )
    ys = [far, forwarded, left1, paired, right1]
    x_re = spec[:, :, :windows]
    x_im = spec[:, :, windows:]
    lx = jnp.concatenate([spec, jnp.concatenate([-x_im, x_re], axis=2)], axis=1)
    result = cross_block(partner_row, counts, lx, ys, windows, slots)
    return result[None]


def solution(mesh):
    in_specs = (P("sta", "tm", None), P("sta", None), P("sta"))
    out_specs = P("sta", None, None, "tm")
    return jax.shard_map(body, mesh=mesh, in_specs=in_specs, out_specs=out_specs, check_vma=False)
```

```python
import math

import jax
import numpy as np
import jax.numpy as jnp
from jax import lax
from jax.experimental import pallas as pl
from jax.experimental.pallas import tpu as pltpu
from jax.sharding import PartitionSpec as P

BINS = 128
R = 2
BINS_PER_STEP = 8


def passed_along(array, axis, by, sources=lambda i: True):
    peers = lax.axis_size(axis)
    pairs = [(i, i + by) for i in range(peers) if 0 <= i + by < peers and sources(i)]
    return lax.ppermute(array, axis, pairs)


def dft_factors(samples, bins, groups):
    local = bins // groups
    column = np.arange(2 * bins)
    group_of = column // (2 * local)
    part_of = column // local % 2
    harmonic = group_of * local + column % local + 1
    fine = 1 << ((samples.bit_length() - 1) // 2)
    coarse = samples // fine
    unit = 2.0 * math.pi / samples
    outer = (np.arange(coarse)[:, None] * fine * harmonic[None, :]) % samples * unit
    inner = (np.arange(fine)[:, None] * harmonic[None, :]) % samples * unit
    is_cos = part_of[None, :] == 0
    p1 = np.where(is_cos, np.cos(outer), -np.sin(outer))
    q1 = np.where(is_cos, -np.sin(outer), -np.cos(outer))
    c2 = np.cos(inner)
    s2 = np.sin(inner)
    return tuple(jnp.asarray(t.astype(np.float32)) for t in (p1, q1, c2, s2))


def split_bf16(v):
    hi = v.astype(jnp.bfloat16)
    lo = (v - hi.astype(jnp.float32)).astype(jnp.bfloat16)
    return hi, lo


def dft_kernel(p1_ref, q1_ref, c2_ref, s2_ref, x_ref, o_ref, acc_ref):
    k = pl.program_id(0)

    @pl.when(k == 0)
    def _():
        acc_ref[...] = jnp.zeros(acc_ref.shape, acc_ref.dtype)

    c2 = c2_ref[...]
    s2 = s2_ref[...]
    rows = [p1_ref[a:a + 1, :] * c2 + q1_ref[a:a + 1, :] * s2 for a in range(p1_ref.shape[0])]
    t_hi, t_lo = split_bf16(jnp.concatenate(rows, axis=0))
    x_hi, x_lo = split_bf16(x_ref[...])
    dot = lambda a, b: jnp.dot(a, b, preferred_element_type=jnp.float32)
    acc_ref[...] += dot(x_hi, t_hi) + dot(x_hi, t_lo) + dot(x_lo, t_hi)

    @pl.when(k == pl.num_programs(0) - 1)
    def _():
        spectra = acc_ref[...]
        mean_power = jnp.mean(spectra * spectra, axis=1, keepdims=True)
        o_ref[...] = (spectra / jnp.sqrt(mean_power + 1e-06)).astype(o_ref.dtype)


def whiten(records, groups):
    stations, windows, samples = records.shape
    p1, q1, c2, s2 = dft_factors(samples, BINS, groups)
    fine, width = c2.shape
    coarse_step = 32
    rows = stations * windows
    x = records.reshape(rows, samples)
    white = pl.pallas_call(
        dft_kernel,
        grid=(samples // (fine * coarse_step),),
        in_specs=[
            pl.BlockSpec((coarse_step, width), lambda k: (k, 0)),
            pl.BlockSpec((coarse_step, width), lambda k: (k, 0)),
            pl.BlockSpec((fine, width), lambda k: (0, 0)),
            pl.BlockSpec((fine, width), lambda k: (0, 0)),
            pl.BlockSpec((rows, fine * coarse_step), lambda k: (0, k)),
        ],
        out_specs=pl.BlockSpec((rows, width), lambda k: (0, 0)),
        out_shape=jax.ShapeDtypeStruct((rows, width), jnp.bfloat16),
        scratch_shapes=[pltpu.VMEM((rows, width), jnp.float32)],
    )(p1, q1, c2, s2, x)
    return white.reshape(1, stations, windows, groups, width // groups)


def cross_kernel(scale, partner_ref, count_ref, lx_ref, *refs):
    *y_refs, o_ref = refs
    bins, two_s, _ = lx_ref.shape
    s = two_s // 2
    slots = o_ref.shape[0]
    block_index = lax.axis_index("sta")
    parity = block_index % 2
    sel = []
    for p in range(slots):
        where_at = jnp.clip(partner_ref[p] - block_index + R, 0, 2 * R)
        slot = jnp.where(where_at == 0, parity, where_at + 1)
        slot = jnp.where(where_at == 2 * R, 1 - parity, slot)
        sel.append(jnp.where(p < count_ref[0], slot, -1))
    for j in range(bins // 2):
        picked = []
        for p in range(slots):
            y = jnp.zeros(y_refs[0].shape[1:], y_refs[0].dtype)
            for o, y_ref in enumerate(y_refs):
                y = jnp.where(sel[p] == o, y_ref[j], y)
            picked.append(y)
        ycat = jnp.concatenate(picked, axis=0)
        for h in range(2):
            b = 2 * j + h
            r = lax.dot_general(
                lx_ref[b], ycat, (((1,), (1,)), ((), ())), preferred_element_type=jnp.float32
            )
            r = r * scale
            for p in range(slots):
                src = (2 * p + h) * s
                for x in range(2):
                    col = (2 * b + x) * s
                    o_ref[p, :, col:col + s] = r[x * s:(x + 1) * s, src:src + s]


def cross_block(partner_row, count, lx, ys, windows, slots):
    nb, two_s, k = lx.shape
    s = two_s // 2
    step = BINS_PER_STEP
    kernel = lambda *refs: cross_kernel(1.0 / windows, *refs)
    y_spec = pl.BlockSpec((step // 2, two_s, k), lambda g, *_: (g, 0, 0))
    grid_spec = pltpu.PrefetchScalarGridSpec(
        num_scalar_prefetch=2,
        grid=(nb // step,),
        in_specs=[pl.BlockSpec((step, two_s, k), lambda g, *_: (g, 0, 0))] + [y_spec] * len(ys),
        out_specs=pl.BlockSpec((slots, s, step * two_s), lambda g, *_: (0, 0, g)),
    )
    return pl.pallas_call(
        kernel,
        grid_spec=grid_spec,
        out_shape=jax.ShapeDtypeStruct((slots, s, nb * two_s), jnp.float32),
    )(partner_row, count, lx, *ys)


def body(records, partners, counts):
    own_spec = whiten(records, lax.axis_size("tm"))
    block_index = lax.axis_index("sta")
    partner_row = partners[0]
    slots = partner_row.shape[0]
    live_slots = jnp.arange(slots, dtype=jnp.int32) < counts[0]
    regrouped = lax.all_to_all(own_spec, "tm", split_axis=3, concat_axis=2, tiled=True)
    stations, windows, width = regrouped.shape[1], regrouped.shape[2], regrouped.shape[4]
    nb = width // 2
    spec = (
        regrouped.reshape(stations, windows, 2, nb)
        .transpose(3, 0, 1, 2)
        .reshape(nb, stations, 2 * windows)
    )
    paired = spec.reshape(nb // 2, 2 * stations, 2 * windows)
    peers = lax.axis_size("sta")
    parity = block_index % 2
    left1 = passed_along(paired, "sta", 1)
    right1 = passed_along(paired, "sta", -1)
    far = lax.ppermute(
        paired, "sta", [(i, i + 2 - 4 * (i % 2)) for i in range(peers) if 0 <= i + 2 - 4 * (i % 2) < peers]
    )
    relay = jnp.where(parity == 0, left1, right1)
    forwarded = lax.ppermute(
        relay, "sta", [(i, i + 1 - 2 * (i % 2)) for i in range(peers) if 0 <= i + 1 - 2 * (i % 2) < peers]
    )
    ys = [far, forwarded, left1, paired, right1]
    pairs_view = spec.reshape(nb, stations, windows, 2)
    x_re = pairs_view[..., 0]
    x_im = pairs_view[..., 1]
    swapped = jnp.stack([-x_im, x_re], axis=3).reshape(nb, stations, 2 * windows)
    lx = jnp.concatenate([spec, swapped], axis=1)
    result = cross_block(partner_row, counts, lx, ys, windows, slots)
    return result[None]


def solution(mesh):
    in_specs = (P("sta", "tm", None), P("sta", None), P("sta"))
    out_specs = P("sta", None, None, "tm")
    return jax.shard_map(body, mesh=mesh, in_specs=in_specs, out_specs=out_specs, check_vma=False)
```

```python
import math

import jax
import numpy as np
import jax.numpy as jnp
from jax import lax
from jax.experimental import pallas as pl
from jax.experimental.pallas import tpu as pltpu
from jax.sharding import PartitionSpec as P

BINS = 128
R = 2
BINS_PER_STEP = 8


def passed_along(array, axis, by, sources=lambda i: True):
    peers = lax.axis_size(axis)
    pairs = [(i, i + by) for i in range(peers) if 0 <= i + by < peers and sources(i)]
    return lax.ppermute(array, axis, pairs)


def dft_factors(samples, bins, groups):
    local = bins // groups
    column = np.arange(2 * bins)
    group_of = column // (2 * local)
    part_of = column // local % 2
    harmonic = group_of * local + column % local + 1
    fine = 1 << ((samples.bit_length() - 1) // 2)
    coarse = samples // fine
    unit = 2.0 * math.pi / samples
    outer = (np.arange(coarse)[:, None] * fine * harmonic[None, :]) % samples * unit
    inner = (np.arange(fine)[:, None] * harmonic[None, :]) % samples * unit
    is_cos = part_of[None, :] == 0
    p1 = np.where(is_cos, np.cos(outer), -np.sin(outer))
    q1 = np.where(is_cos, -np.sin(outer), -np.cos(outer))
    c2 = np.cos(inner)
    s2 = np.sin(inner)
    return tuple(jnp.asarray(t.astype(np.float32)) for t in (p1, q1, c2, s2))


def split_bf16(v):
    hi = v.astype(jnp.bfloat16)
    lo = (v - hi.astype(jnp.float32)).astype(jnp.bfloat16)
    return hi, lo


def dft_kernel(p1_ref, q1_ref, c2_ref, s2_ref, x_ref, o_ref, acc_ref):
    k = pl.program_id(0)

    @pl.when(k == 0)
    def _():
        acc_ref[...] = jnp.zeros(acc_ref.shape, acc_ref.dtype)

    c2 = c2_ref[...]
    s2 = s2_ref[...]
    rows = [p1_ref[a:a + 1, :] * c2 + q1_ref[a:a + 1, :] * s2 for a in range(p1_ref.shape[0])]
    t_hi, t_lo = split_bf16(jnp.concatenate(rows, axis=0))
    x_hi, x_lo = split_bf16(x_ref[...])
    dot = lambda a, b: jnp.dot(a, b, preferred_element_type=jnp.float32)
    acc_ref[...] += dot(x_hi, t_hi) + dot(x_hi, t_lo) + dot(x_lo, t_hi)

    @pl.when(k == pl.num_programs(0) - 1)
    def _():
        spectra = acc_ref[...]
        mean_power = jnp.mean(spectra * spectra, axis=1, keepdims=True)
        o_ref[...] = (spectra / jnp.sqrt(mean_power + 1e-06)).astype(o_ref.dtype)


def whiten(records, groups):
    stations, windows, samples = records.shape
    p1, q1, c2, s2 = dft_factors(samples, BINS, groups)
    fine, width = c2.shape
    coarse_step = 32
    rows = stations * windows
    x = records.reshape(rows, samples)
    white = pl.pallas_call(
        dft_kernel,
        grid=(samples // (fine * coarse_step),),
        in_specs=[
            pl.BlockSpec((coarse_step, width), lambda k: (k, 0)),
            pl.BlockSpec((coarse_step, width), lambda k: (k, 0)),
            pl.BlockSpec((fine, width), lambda k: (0, 0)),
            pl.BlockSpec((fine, width), lambda k: (0, 0)),
            pl.BlockSpec((rows, fine * coarse_step), lambda k: (0, k)),
        ],
        out_specs=pl.BlockSpec((rows, width), lambda k: (0, 0)),
        out_shape=jax.ShapeDtypeStruct((rows, width), jnp.bfloat16),
        scratch_shapes=[pltpu.VMEM((rows, width), jnp.float32)],
    )(p1, q1, c2, s2, x)
    return white.reshape(1, stations, windows, groups, width // groups)


def cross_kernel(scale, partner_ref, count_ref, lx_ref, *refs):
    *y_refs, o_ref = refs
    bins, two_s, _ = lx_ref.shape
    s = two_s // 2
    slots = o_ref.shape[0]
    block_index = lax.axis_index("sta")
    parity = block_index % 2
    sel = []
    for p in range(slots):
        where_at = jnp.clip(partner_ref[p] - block_index + R, 0, 2 * R)
        slot = jnp.where(where_at == 0, parity, where_at + 1)
        slot = jnp.where(where_at == 2 * R, 1 - parity, slot)
        sel.append(jnp.where(p < count_ref[0], slot, -1))
    for b in range(bins):
        picked = []
        for p in range(slots):
            y = jnp.zeros(y_refs[0].shape[1:], y_refs[0].dtype)
            for o, y_ref in enumerate(y_refs):
                y = jnp.where(sel[p] == o, y_ref[b], y)
            picked.append(y.astype(jnp.float32))
        ycat = jnp.concatenate(picked, axis=0).astype(lx_ref.dtype)
        r = lax.dot_general(
            lx_ref[b], ycat, (((1,), (1,)), ((), ())), preferred_element_type=jnp.float32
        )
        r = r * scale
        for p in range(slots):
            for x in range(2):
                col = (2 * b + x) * s
                o_ref[p, :, col:col + s] = r[x * s:(x + 1) * s, p * s:(p + 1) * s]


def cross_block(partner_row, count, lx, ys, windows, slots):
    nb, two_s, k = lx.shape
    s = two_s // 2
    step = BINS_PER_STEP
    kernel = lambda *refs: cross_kernel(1.0 / windows, *refs)
    y_spec = pl.BlockSpec((step, s, k), lambda g, *_: (g, 0, 0))
    grid_spec = pltpu.PrefetchScalarGridSpec(
        num_scalar_prefetch=2,
        grid=(nb // step,),
        in_specs=[pl.BlockSpec((step, two_s, k), lambda g, *_: (g, 0, 0))] + [y_spec] * len(ys),
        out_specs=pl.BlockSpec((slots, s, step * two_s), lambda g, *_: (0, 0, g)),
    )
    return pl.pallas_call(
        kernel,
        grid_spec=grid_spec,
        out_shape=jax.ShapeDtypeStruct((slots, s, nb * two_s), jnp.float32),
    )(partner_row, count, lx, *ys)


def body(records, partners, counts):
    own_spec = whiten(records, lax.axis_size("tm"))
    block_index = lax.axis_index("sta")
    partner_row = partners[0]
    slots = partner_row.shape[0]
    live_slots = jnp.arange(slots, dtype=jnp.int32) < counts[0]
    regrouped = lax.all_to_all(own_spec, "tm", split_axis=3, concat_axis=2, tiled=True)
    stations, windows, width = regrouped.shape[1], regrouped.shape[2], regrouped.shape[4]
    nb = width // 2
    spec = (
        regrouped.reshape(stations, windows, 2, nb)
        .transpose(3, 0, 1, 2)
        .reshape(nb, stations, 2 * windows)
    )
    paired = spec
    peers = lax.axis_size("sta")
    parity = block_index % 2
    left1 = passed_along(paired, "sta", 1)
    right1 = passed_along(paired, "sta", -1)
    far = lax.ppermute(
        paired, "sta", [(i, i + 2 - 4 * (i % 2)) for i in range(peers) if 0 <= i + 2 - 4 * (i % 2) < peers]
    )
    relay = jnp.where(parity == 0, left1, right1)
    forwarded = lax.ppermute(
        relay, "sta", [(i, i + 1 - 2 * (i % 2)) for i in range(peers) if 0 <= i + 1 - 2 * (i % 2) < peers]
    )
    ys = [far, forwarded, left1, paired, right1]
    pairs_view = spec.reshape(nb, stations, windows, 2)
    x_re = pairs_view[..., 0]
    x_im = pairs_view[..., 1]
    swapped = jnp.stack([-x_im, x_re], axis=3).reshape(nb, stations, 2 * windows)
    lx = jnp.concatenate([spec, swapped], axis=1)
    result = cross_block(partner_row, counts, lx, ys, windows, slots)
    return result[None]


def solution(mesh):
    in_specs = (P("sta", "tm", None), P("sta", None), P("sta"))
    out_specs = P("sta", None, None, "tm")
    return jax.shard_map(body, mesh=mesh, in_specs=in_specs, out_specs=out_specs, check_vma=False)
```

```python
import math

import jax
import numpy as np
import jax.numpy as jnp
from jax import lax
from jax.experimental import pallas as pl
from jax.experimental.pallas import tpu as pltpu
from jax.sharding import PartitionSpec as P

BINS = 128
R = 2
BINS_PER_STEP = 16


def passed_along(array, axis, by, sources=lambda i: True):
    peers = lax.axis_size(axis)
    pairs = [(i, i + by) for i in range(peers) if 0 <= i + by < peers and sources(i)]
    return lax.ppermute(array, axis, pairs)


def dft_factors(samples, bins, groups):
    local = bins // groups
    column = np.arange(2 * bins)
    group_of = column // (2 * local)
    part_of = column // local % 2
    harmonic = group_of * local + column % local + 1
    fine = 1 << ((samples.bit_length() - 1) // 2)
    coarse = samples // fine
    unit = 2.0 * math.pi / samples
    outer = (np.arange(coarse)[:, None] * fine * harmonic[None, :]) % samples * unit
    inner = (np.arange(fine)[:, None] * harmonic[None, :]) % samples * unit
    is_cos = part_of[None, :] == 0
    p1 = np.where(is_cos, np.cos(outer), -np.sin(outer))
    q1 = np.where(is_cos, -np.sin(outer), -np.cos(outer))
    c2 = np.cos(inner)
    s2 = np.sin(inner)
    return tuple(jnp.asarray(t.astype(np.float32)) for t in (p1, q1, c2, s2))


def split_bf16(v):
    hi = v.astype(jnp.bfloat16)
    lo = (v - hi.astype(jnp.float32)).astype(jnp.bfloat16)
    return hi, lo


def dft_kernel(p1_ref, q1_ref, c2_ref, s2_ref, x_ref, o_ref, acc_ref):
    k = pl.program_id(0)

    @pl.when(k == 0)
    def _():
        acc_ref[...] = jnp.zeros(acc_ref.shape, acc_ref.dtype)

    c2 = c2_ref[...]
    s2 = s2_ref[...]
    rows = [p1_ref[a:a + 1, :] * c2 + q1_ref[a:a + 1, :] * s2 for a in range(p1_ref.shape[0])]
    t_hi, t_lo = split_bf16(jnp.concatenate(rows, axis=0))
    x_hi, x_lo = split_bf16(x_ref[...])
    dot = lambda a, b: jnp.dot(a, b, preferred_element_type=jnp.float32)
    acc_ref[...] += dot(x_hi, t_hi) + dot(x_hi, t_lo) + dot(x_lo, t_hi)

    @pl.when(k == pl.num_programs(0) - 1)
    def _():
        spectra = acc_ref[...]
        mean_power = jnp.mean(spectra * spectra, axis=1, keepdims=True)
        o_ref[...] = (spectra / jnp.sqrt(mean_power + 1e-06)).astype(o_ref.dtype)


def whiten(records, groups):
    stations, windows, samples = records.shape
    p1, q1, c2, s2 = dft_factors(samples, BINS, groups)
    fine, width = c2.shape
    coarse_step = 32
    rows = stations * windows
    x = records.reshape(rows, samples)
    white = pl.pallas_call(
        dft_kernel,
        grid=(samples // (fine * coarse_step),),
        in_specs=[
            pl.BlockSpec((coarse_step, width), lambda k: (k, 0)),
            pl.BlockSpec((coarse_step, width), lambda k: (k, 0)),
            pl.BlockSpec((fine, width), lambda k: (0, 0)),
            pl.BlockSpec((fine, width), lambda k: (0, 0)),
            pl.BlockSpec((rows, fine * coarse_step), lambda k: (0, k)),
        ],
        out_specs=pl.BlockSpec((rows, width), lambda k: (0, 0)),
        out_shape=jax.ShapeDtypeStruct((rows, width), jnp.bfloat16),
        scratch_shapes=[pltpu.VMEM((rows, width), jnp.float32)],
    )(p1, q1, c2, s2, x)
    return white.reshape(1, stations, windows, groups, width // groups)


def cross_kernel(scale, partner_ref, count_ref, lx_ref, *refs):
    *y_refs, o_ref = refs
    bins, two_s, _ = lx_ref.shape
    s = two_s // 2
    slots = o_ref.shape[0]
    block_index = lax.axis_index("sta")
    parity = block_index % 2
    sel = []
    for p in range(slots):
        where_at = jnp.clip(partner_ref[p] - block_index + R, 0, 2 * R)
        slot = jnp.where(where_at == 0, parity, where_at + 1)
        slot = jnp.where(where_at == 2 * R, 1 - parity, slot)
        sel.append(jnp.where(p < count_ref[0], slot, -1))
    for b in range(bins):
        picked = []
        for p in range(slots):
            y = jnp.zeros(y_refs[0].shape[1:], y_refs[0].dtype)
            for o, y_ref in enumerate(y_refs):
                y = jnp.where(sel[p] == o, y_ref[b], y)
            picked.append(y.astype(jnp.float32))
        ycat = jnp.concatenate(picked, axis=0).astype(lx_ref.dtype)
        r = lax.dot_general(
            lx_ref[b], ycat, (((1,), (1,)), ((), ())), preferred_element_type=jnp.float32
        )
        for p in range(slots):
            for x in range(2):
                col = (2 * b + x) * s
                o_ref[p, :, col:col + s] = r[x * s:(x + 1) * s, p * s:(p + 1) * s]


def cross_block(partner_row, count, lx, ys, windows, slots):
    nb, two_s, k = lx.shape
    s = two_s // 2
    step = BINS_PER_STEP
    kernel = lambda *refs: cross_kernel(1.0 / windows, *refs)
    y_spec = pl.BlockSpec((step, s, k), lambda g, *_: (g, 0, 0))
    grid_spec = pltpu.PrefetchScalarGridSpec(
        num_scalar_prefetch=2,
        grid=(nb // step,),
        in_specs=[pl.BlockSpec((step, two_s, k), lambda g, *_: (g, 0, 0))] + [y_spec] * len(ys),
        out_specs=pl.BlockSpec((slots, s, step * two_s), lambda g, *_: (0, 0, g)),
    )
    return pl.pallas_call(
        kernel,
        grid_spec=grid_spec,
        out_shape=jax.ShapeDtypeStruct((slots, s, nb * two_s), jnp.float32),
    )(partner_row, count, lx, *ys)


def body(records, partners, counts):
    own_spec = whiten(records, lax.axis_size("tm"))
    block_index = lax.axis_index("sta")
    partner_row = partners[0]
    slots = partner_row.shape[0]
    live_slots = jnp.arange(slots, dtype=jnp.int32) < counts[0]
    regrouped = lax.all_to_all(own_spec, "tm", split_axis=3, concat_axis=2, tiled=True)
    stations, windows, width = regrouped.shape[1], regrouped.shape[2], regrouped.shape[4]
    nb = width // 2
    spec = (
        regrouped.reshape(stations, windows, 2, nb)
        .transpose(3, 0, 1, 2)
        .reshape(nb, stations, 2 * windows)
    )
    paired = spec
    peers = lax.axis_size("sta")
    parity = block_index % 2
    left1 = passed_along(paired, "sta", 1)
    right1 = passed_along(paired, "sta", -1)
    far = lax.ppermute(
        paired, "sta", [(i, i + 2 - 4 * (i % 2)) for i in range(peers) if 0 <= i + 2 - 4 * (i % 2) < peers]
    )
    relay = jnp.where(parity == 0, left1, right1)
    forwarded = lax.ppermute(
        relay, "sta", [(i, i + 1 - 2 * (i % 2)) for i in range(peers) if 0 <= i + 1 - 2 * (i % 2) < peers]
    )
    ys = [far, forwarded, left1, paired, right1]
    pairs_view = spec.reshape(nb, stations, windows, 2)
    x_re = pairs_view[..., 0]
    x_im = pairs_view[..., 1]
    swapped = jnp.stack([-x_im, x_re], axis=3).reshape(nb, stations, 2 * windows)
    lx = jnp.concatenate([spec, swapped], axis=1)
    lx = lx * jnp.asarray(1.0 / windows, lx.dtype)
    result = cross_block(partner_row, counts, lx, ys, windows, slots)
    return result[None]


def solution(mesh):
    in_specs = (P("sta", "tm", None), P("sta", None), P("sta"))
    out_specs = P("sta", None, None, "tm")
    return jax.shard_map(body, mesh=mesh, in_specs=in_specs, out_specs=out_specs, check_vma=False)
```

```python
import math

import jax
import numpy as np
import jax.numpy as jnp
from jax import lax
from jax.experimental import pallas as pl
from jax.experimental.pallas import tpu as pltpu
from jax.sharding import PartitionSpec as P

BINS = 128
R = 2
BINS_PER_STEP = 16


def passed_along(array, axis, by, sources=lambda i: True):
    peers = lax.axis_size(axis)
    pairs = [(i, i + by) for i in range(peers) if 0 <= i + by < peers and sources(i)]
    return lax.ppermute(array, axis, pairs)


def dft_factors(samples, bins, groups):
    local = bins // groups
    column = np.arange(2 * bins)
    group_of = column // (2 * local)
    part_of = column // local % 2
    harmonic = group_of * local + column % local + 1
    fine = 1 << ((samples.bit_length() - 1) // 2)
    coarse = samples // fine
    unit = 2.0 * math.pi / samples
    outer = (np.arange(coarse)[:, None] * fine * harmonic[None, :]) % samples * unit
    inner = (np.arange(fine)[:, None] * harmonic[None, :]) % samples * unit
    is_cos = part_of[None, :] == 0
    p1 = np.where(is_cos, np.cos(outer), -np.sin(outer))
    q1 = np.where(is_cos, -np.sin(outer), -np.cos(outer))
    c2 = np.cos(inner)
    s2 = np.sin(inner)
    return tuple(jnp.asarray(t.astype(np.float32)) for t in (p1, q1, c2, s2))


def split_bf16(v):
    hi = v.astype(jnp.bfloat16)
    lo = (v - hi.astype(jnp.float32)).astype(jnp.bfloat16)
    return hi, lo


def dft_kernel(p1_ref, q1_ref, c2_ref, s2_ref, x_ref, o_ref, acc_ref, th_ref, tl_ref):
    k = pl.program_id(0)
    i = pl.program_id(1)
    rows = x_ref.shape[0]
    here = pl.ds(pl.multiple_of(i * rows, rows), rows)

    @pl.when(i == 0)
    def _():
        c2 = c2_ref[...]
        s2 = s2_ref[...]
        parts = [p1_ref[a:a + 1, :] * c2 + q1_ref[a:a + 1, :] * s2 for a in range(p1_ref.shape[0])]
        t_hi, t_lo = split_bf16(jnp.concatenate(parts, axis=0))
        th_ref[...] = t_hi
        tl_ref[...] = t_lo

    @pl.when(k == 0)
    def _():
        acc_ref[here, :] = jnp.zeros((rows, acc_ref.shape[1]), acc_ref.dtype)

    x_hi, x_lo = split_bf16(x_ref[...])
    t_hi = th_ref[...]
    dot = lambda a, b: jnp.dot(a, b, preferred_element_type=jnp.float32)
    acc_ref[here, :] += dot(x_hi, t_hi) + dot(x_hi, tl_ref[...]) + dot(x_lo, t_hi)

    @pl.when(k == pl.num_programs(0) - 1)
    def _():
        spectra = acc_ref[here, :]
        mean_power = jnp.mean(spectra * spectra, axis=1, keepdims=True)
        o_ref[...] = (spectra / jnp.sqrt(mean_power + 1e-06)).astype(o_ref.dtype)


def whiten(records, groups):
    stations, windows, samples = records.shape
    p1, q1, c2, s2 = dft_factors(samples, BINS, groups)
    fine, width = c2.shape
    coarse_step = 32
    rows = stations * windows
    x = records.reshape(rows, samples)
    halves = 2
    block = fine * coarse_step
    white = pl.pallas_call(
        dft_kernel,
        grid=(samples // block, halves),
        in_specs=[
            pl.BlockSpec((coarse_step, width), lambda k, i: (k, 0)),
            pl.BlockSpec((coarse_step, width), lambda k, i: (k, 0)),
            pl.BlockSpec((fine, width), lambda k, i: (0, 0)),
            pl.BlockSpec((fine, width), lambda k, i: (0, 0)),
            pl.BlockSpec((rows // halves, block), lambda k, i: (i, k)),
        ],
        out_specs=pl.BlockSpec((rows // halves, width), lambda k, i: (i, 0)),
        out_shape=jax.ShapeDtypeStruct((rows, width), jnp.bfloat16),
        scratch_shapes=[
            pltpu.VMEM((rows, width), jnp.float32),
            pltpu.VMEM((block, width), jnp.bfloat16),
            pltpu.VMEM((block, width), jnp.bfloat16),
        ],
    )(p1, q1, c2, s2, x)
    return white.reshape(1, stations, windows, groups, width // groups)


def cross_kernel(scale, partner_ref, count_ref, lx_ref, *refs):
    *y_refs, o_ref = refs
    bins, two_s, _ = lx_ref.shape
    s = two_s // 2
    slots = o_ref.shape[0]
    block_index = lax.axis_index("sta")
    parity = block_index % 2
    sel = []
    for p in range(slots):
        where_at = jnp.clip(partner_ref[p] - block_index + R, 0, 2 * R)
        slot = jnp.where(where_at == 0, parity, where_at + 1)
        slot = jnp.where(where_at == 2 * R, 1 - parity, slot)
        sel.append(jnp.where(p < count_ref[0], slot, -1))
    for b in range(bins):
        picked = []
        for p in range(slots):
            y = jnp.zeros(y_refs[0].shape[1:], y_refs[0].dtype)
            for o, y_ref in enumerate(y_refs):
                y = jnp.where(sel[p] == o, y_ref[b], y)
            picked.append(y.astype(jnp.float32))
        ycat = jnp.concatenate(picked, axis=0).astype(lx_ref.dtype)
        r = lax.dot_general(
            lx_ref[b], ycat, (((1,), (1,)), ((), ())), preferred_element_type=jnp.float32
        )
        for p in range(slots):
            for x in range(2):
                col = (2 * b + x) * s
                o_ref[p, :, col:col + s] = r[x * s:(x + 1) * s, p * s:(p + 1) * s]


def cross_block(partner_row, count, lx, ys, windows, slots):
    nb, two_s, k = lx.shape
    s = two_s // 2
    step = BINS_PER_STEP
    kernel = lambda *refs: cross_kernel(1.0 / windows, *refs)
    y_spec = pl.BlockSpec((step, s, k), lambda g, *_: (g, 0, 0))
    grid_spec = pltpu.PrefetchScalarGridSpec(
        num_scalar_prefetch=2,
        grid=(nb // step,),
        in_specs=[pl.BlockSpec((step, two_s, k), lambda g, *_: (g, 0, 0))] + [y_spec] * len(ys),
        out_specs=pl.BlockSpec((slots, s, step * two_s), lambda g, *_: (0, 0, g)),
    )
    return pl.pallas_call(
        kernel,
        grid_spec=grid_spec,
        out_shape=jax.ShapeDtypeStruct((slots, s, nb * two_s), jnp.float32),
    )(partner_row, count, lx, *ys)


def body(records, partners, counts):
    own_spec = whiten(records, lax.axis_size("tm"))
    block_index = lax.axis_index("sta")
    partner_row = partners[0]
    slots = partner_row.shape[0]
    live_slots = jnp.arange(slots, dtype=jnp.int32) < counts[0]
    regrouped = lax.all_to_all(own_spec, "tm", split_axis=3, concat_axis=2, tiled=True)
    stations, windows, width = regrouped.shape[1], regrouped.shape[2], regrouped.shape[4]
    nb = width // 2
    spec = (
        regrouped.reshape(stations, windows, 2, nb)
        .transpose(3, 0, 1, 2)
        .reshape(nb, stations, 2 * windows)
    )
    paired = spec
    peers = lax.axis_size("sta")
    parity = block_index % 2
    left1 = passed_along(paired, "sta", 1)
    right1 = passed_along(paired, "sta", -1)
    far = lax.ppermute(
        paired, "sta", [(i, i + 2 - 4 * (i % 2)) for i in range(peers) if 0 <= i + 2 - 4 * (i % 2) < peers]
    )
    relay = jnp.where(parity == 0, left1, right1)
    forwarded = lax.ppermute(
        relay, "sta", [(i, i + 1 - 2 * (i % 2)) for i in range(peers) if 0 <= i + 1 - 2 * (i % 2) < peers]
    )
    ys = [far, forwarded, left1, paired, right1]
    pairs_view = spec.reshape(nb, stations, windows, 2)
    x_re = pairs_view[..., 0]
    x_im = pairs_view[..., 1]
    swapped = jnp.stack([-x_im, x_re], axis=3).reshape(nb, stations, 2 * windows)
    lx = jnp.concatenate([spec, swapped], axis=1)
    lx = lx * jnp.asarray(1.0 / windows, lx.dtype)
    result = cross_block(partner_row, counts, lx, ys, windows, slots)
    return result[None]


def solution(mesh):
    in_specs = (P("sta", "tm", None), P("sta", None), P("sta"))
    out_specs = P("sta", None, None, "tm")
    return jax.shard_map(body, mesh=mesh, in_specs=in_specs, out_specs=out_specs, check_vma=False)
```

```python
import math

import jax
import numpy as np
import jax.numpy as jnp
from jax import lax
from jax.experimental import pallas as pl
from jax.experimental.pallas import tpu as pltpu
from jax.sharding import PartitionSpec as P

BINS = 128
R = 2
BINS_PER_STEP = 16


def passed_along(array, axis, by, sources=lambda i: True):
    peers = lax.axis_size(axis)
    pairs = [(i, i + by) for i in range(peers) if 0 <= i + by < peers and sources(i)]
    return lax.ppermute(array, axis, pairs)


def dft_factors(samples, bins, groups):
    local = bins // groups
    column = np.arange(2 * bins)
    group_of = column // (2 * local)
    part_of = column // local % 2
    harmonic = group_of * local + column % local + 1
    fine = 1 << ((samples.bit_length() - 1) // 2)
    coarse = samples // fine
    unit = 2.0 * math.pi / samples
    outer = (np.arange(coarse)[:, None] * fine * harmonic[None, :]) % samples * unit
    inner = (np.arange(fine)[:, None] * harmonic[None, :]) % samples * unit
    is_cos = part_of[None, :] == 0
    p1 = np.where(is_cos, np.cos(outer), -np.sin(outer))
    q1 = np.where(is_cos, -np.sin(outer), -np.cos(outer))
    c2 = np.cos(inner)
    s2 = np.sin(inner)
    return tuple(jnp.asarray(t.astype(np.float32)) for t in (p1, q1, c2, s2))


def split_bf16(v):
    hi = v.astype(jnp.bfloat16)
    lo = (v - hi.astype(jnp.float32)).astype(jnp.bfloat16)
    return hi, lo


def dft_kernel(p1_ref, q1_ref, c2_ref, s2_ref, x_ref, o_ref, acc_ref):
    k = pl.program_id(0)

    @pl.when(k == 0)
    def _():
        acc_ref[...] = jnp.zeros(acc_ref.shape, acc_ref.dtype)

    c2 = c2_ref[...]
    s2 = s2_ref[...]
    rows = [p1_ref[a:a + 1, :] * c2 + q1_ref[a:a + 1, :] * s2 for a in range(p1_ref.shape[0])]
    t_hi, t_lo = split_bf16(jnp.concatenate(rows, axis=0))
    x_hi, x_lo = split_bf16(x_ref[...])
    dot = lambda a, b: jnp.dot(a, b, preferred_element_type=jnp.float32)
    acc_ref[...] += dot(x_lo, t_hi)
    acc_ref[...] += dot(x_hi, t_lo)
    acc_ref[...] += dot(x_hi, t_hi)

    @pl.when(k == pl.num_programs(0) - 1)
    def _():
        spectra = acc_ref[...]
        mean_power = jnp.mean(spectra * spectra, axis=1, keepdims=True)
        o_ref[...] = (spectra / jnp.sqrt(mean_power + 1e-06)).astype(o_ref.dtype)


def whiten(records, groups):
    stations, windows, samples = records.shape
    p1, q1, c2, s2 = dft_factors(samples, BINS, groups)
    fine, width = c2.shape
    coarse_step = 32
    rows = stations * windows
    x = records.reshape(rows, samples)
    white = pl.pallas_call(
        dft_kernel,
        grid=(samples // (fine * coarse_step),),
        in_specs=[
            pl.BlockSpec((coarse_step, width), lambda k: (k, 0)),
            pl.BlockSpec((coarse_step, width), lambda k: (k, 0)),
            pl.BlockSpec((fine, width), lambda k: (0, 0)),
            pl.BlockSpec((fine, width), lambda k: (0, 0)),
            pl.BlockSpec((rows, fine * coarse_step), lambda k: (0, k)),
        ],
        out_specs=pl.BlockSpec((rows, width), lambda k: (0, 0)),
        out_shape=jax.ShapeDtypeStruct((rows, width), jnp.bfloat16),
        scratch_shapes=[pltpu.VMEM((rows, width), jnp.float32)],
    )(p1, q1, c2, s2, x)
    return white.reshape(1, stations, windows, groups, width // groups)


def cross_kernel(scale, partner_ref, count_ref, lx_ref, *refs):
    *y_refs, o_ref = refs
    bins, two_s, _ = lx_ref.shape
    s = two_s // 2
    slots = o_ref.shape[0]
    block_index = lax.axis_index("sta")
    parity = block_index % 2
    sel = []
    for p in range(slots):
        where_at = jnp.clip(partner_ref[p] - block_index + R, 0, 2 * R)
        slot = jnp.where(where_at == 0, parity, where_at + 1)
        slot = jnp.where(where_at == 2 * R, 1 - parity, slot)
        sel.append(jnp.where(p < count_ref[0], slot, -1))
    for b in range(bins):
        picked = []
        for p in range(slots):
            y = jnp.zeros(y_refs[0].shape[1:], y_refs[0].dtype)
            for o, y_ref in enumerate(y_refs):
                y = jnp.where(sel[p] == o, y_ref[b], y)
            picked.append(y.astype(jnp.float32))
        ycat = jnp.concatenate(picked, axis=0).astype(lx_ref.dtype)
        r = lax.dot_general(
            lx_ref[b], ycat, (((1,), (1,)), ((), ())), preferred_element_type=jnp.float32
        )
        for p in range(slots):
            for x in range(2):
                col = (2 * b + x) * s
                o_ref[p, :, col:col + s] = r[x * s:(x + 1) * s, p * s:(p + 1) * s]


def cross_block(partner_row, count, lx, ys, windows, slots):
    nb, two_s, k = lx.shape
    s = two_s // 2
    step = BINS_PER_STEP
    kernel = lambda *refs: cross_kernel(1.0 / windows, *refs)
    y_spec = pl.BlockSpec((step, s, k), lambda g, *_: (g, 0, 0))
    grid_spec = pltpu.PrefetchScalarGridSpec(
        num_scalar_prefetch=2,
        grid=(nb // step,),
        in_specs=[pl.BlockSpec((step, two_s, k), lambda g, *_: (g, 0, 0))] + [y_spec] * len(ys),
        out_specs=pl.BlockSpec((slots, s, step * two_s), lambda g, *_: (0, 0, g)),
    )
    return pl.pallas_call(
        kernel,
        grid_spec=grid_spec,
        out_shape=jax.ShapeDtypeStruct((slots, s, nb * two_s), jnp.float32),
    )(partner_row, count, lx, *ys)


def body(records, partners, counts):
    own_spec = whiten(records, lax.axis_size("tm"))
    block_index = lax.axis_index("sta")
    partner_row = partners[0]
    slots = partner_row.shape[0]
    live_slots = jnp.arange(slots, dtype=jnp.int32) < counts[0]
    regrouped = lax.all_to_all(own_spec, "tm", split_axis=3, concat_axis=2, tiled=True)
    stations, windows, width = regrouped.shape[1], regrouped.shape[2], regrouped.shape[4]
    nb = width // 2
    spec = (
        regrouped.reshape(stations, windows, 2, nb)
        .transpose(3, 0, 1, 2)
        .reshape(nb, stations, 2 * windows)
    )
    paired = spec
    peers = lax.axis_size("sta")
    parity = block_index % 2
    left1 = passed_along(paired, "sta", 1)
    right1 = passed_along(paired, "sta", -1)
    far = lax.ppermute(
        paired, "sta", [(i, i + 2 - 4 * (i % 2)) for i in range(peers) if 0 <= i + 2 - 4 * (i % 2) < peers]
    )
    relay = jnp.where(parity == 0, left1, right1)
    forwarded = lax.ppermute(
        relay, "sta", [(i, i + 1 - 2 * (i % 2)) for i in range(peers) if 0 <= i + 1 - 2 * (i % 2) < peers]
    )
    ys = [far, forwarded, left1, paired, right1]
    pairs_view = spec.reshape(nb, stations, windows, 2)
    x_re = pairs_view[..., 0]
    x_im = pairs_view[..., 1]
    swapped = jnp.stack([-x_im, x_re], axis=3).reshape(nb, stations, 2 * windows)
    lx = jnp.concatenate([spec, swapped], axis=1)
    lx = lx * jnp.asarray(1.0 / windows, lx.dtype)
    result = cross_block(partner_row, counts, lx, ys, windows, slots)
    return result[None]


def solution(mesh):
    in_specs = (P("sta", "tm", None), P("sta", None), P("sta"))
    out_specs = P("sta", None, None, "tm")
    return jax.shard_map(body, mesh=mesh, in_specs=in_specs, out_specs=out_specs, check_vma=False)
```

```python
import math

import jax
import numpy as np
import jax.numpy as jnp
from jax import lax
from jax.experimental import pallas as pl
from jax.experimental.pallas import tpu as pltpu
from jax.sharding import PartitionSpec as P

BINS = 128
R = 2
BINS_PER_STEP = 16


def passed_along(array, axis, by, sources=lambda i: True):
    peers = lax.axis_size(axis)
    pairs = [(i, i + by) for i in range(peers) if 0 <= i + by < peers and sources(i)]
    return lax.ppermute(array, axis, pairs)


def dft_factors(samples, bins, groups):
    local = bins // groups
    column = np.arange(2 * bins)
    group_of = column // (2 * local)
    part_of = column // local % 2
    harmonic = group_of * local + column % local + 1
    fine = 1 << ((samples.bit_length() - 1) // 2)
    coarse = samples // fine
    unit = 2.0 * math.pi / samples
    outer = (np.arange(coarse)[:, None] * fine * harmonic[None, :]) % samples * unit
    inner = (np.arange(fine)[:, None] * harmonic[None, :]) % samples * unit
    is_cos = part_of[None, :] == 0
    p1 = np.where(is_cos, np.cos(outer), -np.sin(outer))
    q1 = np.where(is_cos, -np.sin(outer), -np.cos(outer))
    c2 = np.cos(inner)
    s2 = np.sin(inner)
    return tuple(jnp.asarray(t.astype(np.float32)) for t in (p1, q1, c2, s2))


def split_bf16(v):
    hi = v.astype(jnp.bfloat16)
    lo = (v - hi.astype(jnp.float32)).astype(jnp.bfloat16)
    return hi, lo


def dft_kernel(p1_ref, q1_ref, c2_ref, s2_ref, x_ref, o_ref, acc_ref):
    k = pl.program_id(0)

    @pl.when(k == 0)
    def _():
        acc_ref[...] = jnp.zeros(acc_ref.shape, acc_ref.dtype)

    c2 = c2_ref[...]
    s2 = s2_ref[...]
    rows = [p1_ref[a:a + 1, :] * c2 + q1_ref[a:a + 1, :] * s2 for a in range(p1_ref.shape[0])]
    t_hi, t_lo = split_bf16(jnp.concatenate(rows, axis=0))
    x_hi, x_lo = split_bf16(x_ref[...])
    dot = lambda a, b: jnp.dot(a, b, preferred_element_type=jnp.float32)
    acc_ref[...] += dot(x_hi, t_hi) + dot(x_hi, t_lo) + dot(x_lo, t_hi)

    @pl.when(k == pl.num_programs(0) - 1)
    def _():
        spectra = acc_ref[...]
        mean_power = jnp.mean(spectra * spectra, axis=1, keepdims=True)
        o_ref[...] = (spectra / jnp.sqrt(mean_power + 1e-06)).astype(o_ref.dtype)


def whiten(records, groups):
    stations, windows, samples = records.shape
    p1, q1, c2, s2 = dft_factors(samples, BINS, groups)
    fine, width = c2.shape
    coarse_step = 32
    rows = stations * windows
    x = records.reshape(rows, samples)
    white = pl.pallas_call(
        dft_kernel,
        grid=(samples // (fine * coarse_step),),
        in_specs=[
            pl.BlockSpec((coarse_step, width), lambda k: (k, 0)),
            pl.BlockSpec((coarse_step, width), lambda k: (k, 0)),
            pl.BlockSpec((fine, width), lambda k: (0, 0)),
            pl.BlockSpec((fine, width), lambda k: (0, 0)),
            pl.BlockSpec((rows, fine * coarse_step), lambda k: (0, k)),
        ],
        out_specs=pl.BlockSpec((rows, width), lambda k: (0, 0)),
        out_shape=jax.ShapeDtypeStruct((rows, width), jnp.bfloat16),
        scratch_shapes=[pltpu.VMEM((rows, width), jnp.float32)],
    )(p1, q1, c2, s2, x)
    return white.reshape(1, stations, windows, groups, width // groups)


def cross_kernel(scale, partner_ref, count_ref, lx_ref, *refs):
    *y_refs, o_ref = refs
    bins, two_s, _ = lx_ref.shape
    s = two_s // 2
    slots = o_ref.shape[0]
    block_index = lax.axis_index("sta")
    parity = block_index % 2
    sel = []
    for p in range(slots):
        where_at = jnp.clip(partner_ref[p] - block_index + R, 0, 2 * R)
        slot = jnp.where(where_at == 0, parity, where_at + 1)
        slot = jnp.where(where_at == 2 * R, 1 - parity, slot)
        sel.append(jnp.where(p < count_ref[0], slot, -1))
    for b in range(bins):
        picked = []
        for p in range(slots):
            y = jnp.zeros(y_refs[0].shape[1:], y_refs[0].dtype)
            for o, y_ref in enumerate(y_refs):
                y = jnp.where(sel[p] == o, y_ref[b], y)
            picked.append(y.astype(jnp.float32))
        ycat = jnp.concatenate(picked, axis=0).astype(lx_ref.dtype)
        r = lax.dot_general(
            lx_ref[b], ycat, (((1,), (1,)), ((), ())), preferred_element_type=jnp.float32
        )
        for p in range(slots):
            for x in range(2):
                col = (2 * b + x) * s
                o_ref[p, :, col:col + s] = r[x * s:(x + 1) * s, p * s:(p + 1) * s]


def cross_block(partner_row, count, lx, ys, windows, slots):
    nb, two_s, k = lx.shape
    s = two_s // 2
    step = BINS_PER_STEP
    kernel = lambda *refs: cross_kernel(1.0 / windows, *refs)
    y_spec = pl.BlockSpec((step, s, k), lambda g, *_: (g, 0, 0))
    grid_spec = pltpu.PrefetchScalarGridSpec(
        num_scalar_prefetch=2,
        grid=(nb // step,),
        in_specs=[pl.BlockSpec((step, two_s, k), lambda g, *_: (g, 0, 0))] + [y_spec] * len(ys),
        out_specs=pl.BlockSpec((slots, s, step * two_s), lambda g, *_: (0, 0, g)),
    )
    return pl.pallas_call(
        kernel,
        grid_spec=grid_spec,
        out_shape=jax.ShapeDtypeStruct((slots, s, nb * two_s), jnp.float32),
    )(partner_row, count, lx, *ys)


def body(records, partners, counts):
    own_spec = whiten(records, lax.axis_size("tm"))
    block_index = lax.axis_index("sta")
    partner_row = partners[0]
    slots = partner_row.shape[0]
    live_slots = jnp.arange(slots, dtype=jnp.int32) < counts[0]
    regrouped = lax.all_to_all(own_spec, "tm", split_axis=3, concat_axis=2, tiled=True)
    stations, windows, width = regrouped.shape[1], regrouped.shape[2], regrouped.shape[4]
    nb = width // 2
    spec = (
        regrouped.reshape(stations, windows, 2, nb)
        .transpose(3, 0, 1, 2)
        .reshape(nb, stations, 2 * windows)
    )
    paired = spec
    peers = lax.axis_size("sta")
    parity = block_index % 2
    far = lax.ppermute(
        paired, "sta", [(i, i + 2 - 4 * (i % 2)) for i in range(peers) if 0 <= i + 2 - 4 * (i % 2) < peers]
    )
    paired_near, far = lax.optimization_barrier((paired, far))
    left1 = passed_along(paired_near, "sta", 1)
    right1 = passed_along(paired_near, "sta", -1)
    relay = jnp.where(parity == 0, left1, right1)
    forwarded = lax.ppermute(
        relay, "sta", [(i, i + 1 - 2 * (i % 2)) for i in range(peers) if 0 <= i + 1 - 2 * (i % 2) < peers]
    )
    ys = [far, forwarded, left1, paired, right1]
    pairs_view = spec.reshape(nb, stations, windows, 2)
    x_re = pairs_view[..., 0]
    x_im = pairs_view[..., 1]
    swapped = jnp.stack([-x_im, x_re], axis=3).reshape(nb, stations, 2 * windows)
    lx = jnp.concatenate([spec, swapped], axis=1)
    lx = lx * jnp.asarray(1.0 / windows, lx.dtype)
    result = cross_block(partner_row, counts, lx, ys, windows, slots)
    return result[None]


def solution(mesh):
    in_specs = (P("sta", "tm", None), P("sta", None), P("sta"))
    out_specs = P("sta", None, None, "tm")
    return jax.shard_map(body, mesh=mesh, in_specs=in_specs, out_specs=out_specs, check_vma=False)
```
